32 devices in a mesh: parts: 2 (over x), gy: 16 (over z, y, core).
Axes of the slice: x: 2, y: 2, z: 4, core: 2. Of those that a mesh axis runs over, the one named last changes fastest.
Arguments:
- measured: bfloat16 [8, 32, 256, 128], P(None, None, ('parts', 'gy')), parts along dimension 2, may hold values from 0.19921875 to 8
- start: float32 [32, 256, 128], P(None, ('parts', 'gy')), parts along dimension 1, may hold values from 0.5 to 4
- psf: float32 [8, 15, 7, 7], replicated, may hold values from 0.05 to 1
- background: float32 [8], replicated, may hold values from 0.2 to 2
Outputs:
- estimate: float32 [32, 256, 128], P(None, ('parts', 'gy')), parts along dimension 1
The draws below stay inside these ranges and needn't reach their ends.
There are 2 independent parts, one for each index of `parts`. The reference program is written for one: setup_inputs(seed, part) draws one part's arguments, and reference() takes and returns one part's arrays. A program takes and returns all parts, laid end to end along the dimension named above; an argument that names none is the same for every part. Nothing has to cross between parts.
All inputs are finite; a program needn't handle non-finite values.
Results may differ from the reference program's by a relative error of at most 0.0003.
Values may be sent and summed in bfloat16 or wider, within the bound.
No kernel may reach another device: no remote copies, remote signals or barrier semaphores. Data moves between devices by JAX's collectives and lax.ppermute only.
A program may use at most 128 MiB of HBM per device.

```python
import math
import jax
import jax.numpy as jnp
from jax import lax

VIEWS = 8
KZ = 15
KY = 7
KX = 7
PLANES = 32
COLS = 128
ITERS = 1
ROWS = 128


def block_levels(stream_key, dims, cuts, low, high):
    loudness = 1.0
    for dim, shards_of in cuts:
        heights = jax.random.uniform(jax.random.fold_in(jax.random.fold_in(stream_key, 6), dim), (shards_of,), jnp.float32, low / len(cuts), high / len(cuts))
        loudness = loudness * jnp.repeat(jnp.exp(heights), dims[dim] // shards_of).reshape((-1,) + (1,) * (len(dims) - 1 - dim))
    return loudness


def setup_inputs(seed: int = 0, part: int = 0) -> dict:
    splits = jax.random.split(jax.random.key(seed), 5)
    part_keys = jax.random.split(jax.random.fold_in(splits[4], part), 5)
    return {
        "measured": jnp.clip(jnp.exp(math.log(8.0) - 3.6927934 * jax.random.uniform(part_keys[0], (VIEWS, PLANES, ROWS, COLS), jnp.float32) ** block_levels(part_keys[0], (VIEWS, PLANES, ROWS, COLS), ((2, 16),), -0.2, 0.2)), 0.19921875, 8.0).astype(jnp.bfloat16),
        "start": jnp.clip(jnp.exp(math.log(4.0) - 2.0794415 * jax.random.uniform(part_keys[1], (PLANES, ROWS, COLS), jnp.float32) ** block_levels(part_keys[1], (PLANES, ROWS, COLS), ((1, 16),), -0.2, 0.2)), 0.5, 4.0),
        "psf": jnp.clip(jnp.exp(jax.random.uniform(splits[2], (VIEWS, KZ, KY, KX), jnp.float32, math.log(0.05), math.log(1.0))), 0.05, 1.0),
        "background": jnp.clip(jnp.exp(jax.random.uniform(splits[3], (VIEWS,), jnp.float32, math.log(0.2), math.log(2.0))), 0.2, 2.0),
    }


def build_weights(psf, planes):
    kernel = psf / jnp.sum(psf, axis=(1, 2, 3), keepdims=True)
    rounded_kernel = lax.optimization_barrier(kernel.astype(jnp.bfloat16)).astype(jnp.float32)
    depth = psf.shape[1]
    plane_index = jnp.arange(planes, dtype=jnp.int32)
    tap_index = jnp.arange(depth, dtype=jnp.int32)
    onehot = (plane_index[None, :, None] - plane_index[None, None, :] + depth // 2 == tap_index[:, None, None]).astype(jnp.float32)
    views, reach_y, reach_x = psf.shape[0], psf.shape[2], psf.shape[3]
    blur_w = jnp.einsum("vabc,apq->bvpcq", rounded_kernel, onehot, precision=lax.Precision.HIGHEST)
    blur_w = blur_w.reshape(reach_y, views * planes, reach_x * planes).astype(jnp.bfloat16)
    corr_w = jnp.einsum("vabc,apq->vbqcp", rounded_kernel, onehot, precision=lax.Precision.HIGHEST)
    corr_w = corr_w.reshape(views, reach_y, planes, reach_x * planes).astype(jnp.bfloat16)
    return blur_w, corr_w


def column_table(cols, reach_x, sign):
    half_x = reach_x // 2
    source = jnp.arange(cols, dtype=jnp.int32)[:, None, None]
    tap = jnp.arange(reach_x, dtype=jnp.int32)[None, :, None]
    target = jnp.arange(cols, dtype=jnp.int32)[None, None, :]
    table = (source == target + sign * (tap - half_x)).astype(jnp.bfloat16)
    return table.reshape(cols, reach_x * cols)


def blur_rows(padded, blur_w):
    planes, rows_in, cols = padded.shape
    reach_y = blur_w.shape[0]
    reach_x = blur_w.shape[2] // planes
    rows_out = rows_in - 2 * (reach_y // 2)
    table = column_table(cols, reach_x, -1)
    shifted = jnp.dot(padded.reshape(planes * rows_in, cols), table, preferred_element_type=jnp.float32)
    shifted = shifted.astype(jnp.bfloat16).reshape(planes, rows_in, reach_x, cols)
    weights = blur_w.reshape(reach_y, blur_w.shape[1], reach_x, planes)
    result = jnp.zeros((blur_w.shape[1], rows_out, cols), jnp.float32)
    for shift_y in range(reach_y):
        lines = shifted[:, reach_y - 1 - shift_y:reach_y - 1 - shift_y + rows_out]
        result = result + jnp.einsum("ocp,prcx->orx", weights[shift_y], lines, preferred_element_type=jnp.float32)
    return result.reshape(-1, planes, rows_out, cols)


def correlate_rows(padded, corr_w):
    views, planes, rows_in, cols = padded.shape
    reach_y = corr_w.shape[1]
    reach_x = corr_w.shape[3] // planes
    rows_out = rows_in - 2 * (reach_y // 2)
    table = column_table(cols, reach_x, 1)
    shifted = jnp.dot(padded.reshape(views * planes * rows_in, cols), table, preferred_element_type=jnp.float32)
    shifted = shifted.astype(jnp.bfloat16).reshape(views, planes, rows_in, reach_x, cols)
    weights = corr_w.reshape(views, reach_y, planes, reach_x, planes)
    total = jnp.zeros((planes, rows_out, cols), jnp.float32)
    for shift_y in range(reach_y):
        lines = shifted[:, :, shift_y:shift_y + rows_out]
        total = total + jnp.einsum("vqcp,vprcx->qrx", weights[:, shift_y], lines, preferred_element_type=jnp.float32)
    return total


def reference(measured, start, psf, background):
    blur_w, corr_w = build_weights(psf, PLANES)
    half_y = KY // 2
    recorded = measured.astype(jnp.float32)
    estimate = start
    for step in range(ITERS):
        rounded = estimate.astype(jnp.bfloat16)
        padded = jnp.pad(rounded, ((0, 0), (half_y, half_y), (0, 0)))
        blurred = blur_rows(padded, blur_w)
        ratio = (recorded / (blurred + background[:, None, None, None])).astype(jnp.bfloat16)
        ratio_pad = jnp.pad(ratio, ((0, 0), (0, 0), (half_y, half_y), (0, 0)))
        total = correlate_rows(ratio_pad, corr_w)
        estimate = estimate * total / VIEWS
    return estimate
```

```python
import jax
import jax.numpy as jnp
from jax import lax
from jax.experimental import pallas as pl
from jax.experimental.pallas import tpu as pltpu
from jax.sharding import PartitionSpec as P


def halos(x, axis, width):
    peers = lax.axis_size(axis)
    up = [(i, i + 1) for i in range(peers - 1)]
    down = [(j, i) for i, j in up]
    length = x.shape[-1]
    last = x[..., length - width:]
    first = x[..., :width]
    before = lax.ppermute(last, axis, up)
    after = lax.ppermute(first, axis, down)
    return before, after


def build_weights(psf, planes):
    kernel = psf / jnp.sum(psf, axis=(1, 2, 3), keepdims=True)
    rounded_kernel = lax.optimization_barrier(kernel.astype(jnp.bfloat16)).astype(jnp.float32)
    views, depth, reach_y, reach_x = psf.shape
    q = jnp.arange(planes, dtype=jnp.int32)
    tap = jnp.arange(depth, dtype=jnp.int32)
    onehot = (q[None, :, None] - q[None, None, :] + depth // 2 == tap[:, None, None]).astype(jnp.float32)
    blur_w = jnp.einsum("vabc,aqp->bvqcp", rounded_kernel, onehot, precision=lax.Precision.HIGHEST)
    blur_w = blur_w.reshape(reach_y, views * planes, reach_x * planes).astype(jnp.bfloat16)
    corr_w = jnp.einsum("vabc,apq->bcqvp", rounded_kernel, onehot, precision=lax.Precision.HIGHEST)
    corr_w = corr_w.reshape(reach_y, reach_x * planes, views * planes).astype(jnp.bfloat16)
    return blur_w, corr_w


def lane_shift(x, shift, cols):
    n = x.shape[-1]
    rolled = pltpu.roll(x, shift % n, x.ndim - 1) if shift % n else x
    col = lax.broadcasted_iota(jnp.int32, x.shape, x.ndim - 1) % cols
    keep = (col - shift >= 0) & (col - shift < cols)
    return jnp.where(keep, rolled, jnp.zeros_like(rolled))


def blur_kernel(start_ref, lo_ref, hi_ref, w_ref, meas_ref, bg_ref,
                ratio_ref, rlo_ref, rhi_ref, ext_ref, xs_ref, *, cols, reach_y, reach_x, half):
    planes = start_ref.shape[0]
    n_in = ext_ref.shape[1]
    n_out = start_ref.shape[1]
    hw = half * cols
    ext_ref[:, :hw] = lo_ref[...].astype(jnp.float32)
    ext_ref[:, hw:hw + n_out] = start_ref[...].astype(jnp.bfloat16).astype(jnp.float32)
    ext_ref[:, hw + n_out:] = hi_ref[...].astype(jnp.float32)
    ext = ext_ref[...]
    for c in range(reach_x):
        xs_ref[c * planes:(c + 1) * planes, :] = lane_shift(ext, c - reach_x // 2, cols).astype(jnp.bfloat16)
    acc = None
    for b in range(reach_y):
        off = (2 * half - b) * cols
        part = jnp.dot(w_ref[b], xs_ref[:, off:off + n_out], preferred_element_type=jnp.float32)
        acc = part if acc is None else acc + part
    ratio = (meas_ref[...].astype(jnp.float32) / (acc + bg_ref[...])).astype(jnp.bfloat16)
    ratio_ref[...] = ratio
    rlo_ref[...] = ratio[:, :hw]
    rhi_ref[...] = ratio[:, n_out - hw:]


def corr_kernel(ratio_ref, lo_ref, hi_ref, w_ref, est_ref, out_ref, ext_ref, *, cols, reach_y, reach_x, half, views):
    planes = est_ref.shape[0]
    n_out = est_ref.shape[1]
    hw = half * cols
    ext_ref[:, :hw] = lo_ref[...]
    ext_ref[:, hw:hw + n_out] = ratio_ref[...]
    ext_ref[:, hw + n_out:] = hi_ref[...]
    acc = None
    for b in range(reach_y):
        off = b * cols
        part = jnp.dot(w_ref[b], ext_ref[:, off:off + n_out], preferred_element_type=jnp.float32)
        acc = part if acc is None else acc + part
    total = None
    for c in range(reach_x):
        piece = lane_shift(acc[c * planes:(c + 1) * planes], reach_x // 2 - c, cols)
        total = piece if total is None else total + piece
    out_ref[...] = est_ref[...] * total / views


def local(measured, start, psf, background):
    planes, rows, cols = start.shape
    views = measured.shape[0]
    reach_y, reach_x = psf.shape[2], psf.shape[3]
    half = reach_y // 2
    blur_w, corr_w = build_weights(psf, planes)
    n_out = rows * cols
    hw = half * cols
    vmem = pl.BlockSpec(memory_space=pltpu.VMEM)

    start2 = start.reshape(planes, n_out)
    rounded = start2.astype(jnp.bfloat16)
    lo, hi = halos(rounded, "gy", hw)
    meas2 = measured.reshape(views * planes, n_out)
    bg = jnp.broadcast_to(jnp.repeat(background, planes)[:, None], (views * planes, cols))
    bg = jnp.tile(bg, (1, rows))

    ratio, rlo, rhi = pl.pallas_call(
        lambda *refs: blur_kernel(*refs, cols=cols, reach_y=reach_y, reach_x=reach_x, half=half),
        out_shape=(
            jax.ShapeDtypeStruct((views * planes, n_out), jnp.bfloat16),
            jax.ShapeDtypeStruct((views * planes, hw), jnp.bfloat16),
            jax.ShapeDtypeStruct((views * planes, hw), jnp.bfloat16),
        ),
        in_specs=[vmem] * 6,
        out_specs=(vmem, vmem, vmem),
        scratch_shapes=[
            pltpu.VMEM((planes, n_out + 2 * hw), jnp.float32),
            pltpu.VMEM((reach_x * planes, n_out + 2 * hw), jnp.bfloat16),
        ],
    )(start2, lo, hi, blur_w, meas2, bg)

    before = lax.ppermute(rhi, "gy", [(i, i + 1) for i in range(lax.axis_size("gy") - 1)])
    after = lax.ppermute(rlo, "gy", [(i + 1, i) for i in range(lax.axis_size("gy") - 1)])

    est = pl.pallas_call(
        lambda *refs: corr_kernel(*refs, cols=cols, reach_y=reach_y, reach_x=reach_x, half=half, views=views),
        out_shape=jax.ShapeDtypeStruct((planes, n_out), jnp.float32),
        in_specs=[vmem] * 5,
        out_specs=vmem,
        scratch_shapes=[pltpu.VMEM((views * planes, n_out + 2 * hw), jnp.bfloat16)],
    )(ratio, before, after, corr_w, start2)
    return est.reshape(planes, rows, cols)


def solution(mesh):
    in_specs = (P(None, None, ("parts", "gy"), None), P(None, ("parts", "gy"), None), P(), P())
    out_specs = P(None, ("parts", "gy"), None)
    return jax.shard_map(local, mesh=mesh, in_specs=in_specs, out_specs=out_specs, check_vma=False)
```

```python
import jax
import jax.numpy as jnp
from jax import lax
from jax.experimental import pallas as pl
from jax.experimental.pallas import tpu as pltpu
from jax.sharding import PartitionSpec as P


def halos(x, axis, width):
    peers = lax.axis_size(axis)
    up = [(i, i + 1) for i in range(peers - 1)]
    down = [(j, i) for i, j in up]
    length = x.shape[-1]
    last = x[..., length - width:]
    first = x[..., :width]
    before = lax.ppermute(last, axis, up)
    after = lax.ppermute(first, axis, down)
    return before, after


def build_bases(psf, planes, lanes, corr_lanes):
    kernel = psf / jnp.sum(psf, axis=(1, 2, 3), keepdims=True)
    views, depth, reach_y, reach_x = psf.shape
    half_z = depth // 2
    lane = jnp.arange(lanes, dtype=jnp.int32)
    tap = jnp.arange(depth, dtype=jnp.int32)
    col = jnp.arange(reach_x, dtype=jnp.int32)
    at = (col[None, :, None] * planes + half_z - tap[:, None, None]) % lanes
    onehot = (lane[None, None, :] == at).astype(jnp.float32)
    blur = jnp.einsum("vabc,acl->bvl", kernel, onehot, precision=lax.Precision.HIGHEST)
    view = jnp.arange(views, dtype=jnp.int32)
    at = (view[:, None, None] * planes + tap[None, :, None] - half_z) % corr_lanes
    onehot = (jnp.arange(corr_lanes, dtype=jnp.int32)[None, None, :] == at).astype(jnp.float32)
    corr = jnp.einsum("vabc,val->bcl", kernel, onehot, precision=lax.Precision.HIGHEST)
    return blur.astype(jnp.bfloat16), corr.astype(jnp.bfloat16)


def toeplitz_block(row, planes, half_z, width):
    lanes = row.shape[-1]
    blk = jnp.broadcast_to(row, (planes, lanes))
    blk = pltpu.roll(blk, 0, 1, stride=1, stride_axis=0)
    q = lax.broadcasted_iota(jnp.int32, (planes, lanes), 0)
    l = lax.broadcasted_iota(jnp.int32, (planes, lanes), 1)
    d = l % planes - q
    keep = (d <= half_z) & (d >= -half_z) & (l < width)
    return jnp.where(keep, blk, 0.0).astype(jnp.bfloat16)


def lane_shift(x, shift, cols):
    n = x.shape[-1]
    rolled = pltpu.roll(x, shift % n, x.ndim - 1) if shift % n else x
    col = lax.broadcasted_iota(jnp.int32, x.shape, x.ndim - 1) % cols
    keep = (col - shift >= 0) & (col - shift < cols)
    return jnp.where(keep, rolled, jnp.zeros_like(rolled))


def blur_kernel(start_ref, lo_ref, hi_ref, base_ref, meas_ref, bg_ref,
                ratio_ref, rlo_ref, rhi_ref, ext_ref, xs_ref, w_ref, *, cols, reach_y, reach_x, half, half_z):
    planes = start_ref.shape[0]
    n_out = start_ref.shape[1]
    views = base_ref.shape[1]
    hw = half * cols
    width = reach_x * planes
    for b in range(reach_y):
        for v in range(views):
            row = base_ref[b, v:v + 1, :].astype(jnp.float32)
            w_ref[b, v * planes:(v + 1) * planes, :] = toeplitz_block(row, planes, half_z, width)
    xs_ref[width:, :] = jnp.zeros((xs_ref.shape[0] - width, xs_ref.shape[1]), jnp.bfloat16)
    ext_ref[:, :hw] = lo_ref[...].astype(jnp.float32)
    ext_ref[:, hw:hw + n_out] = start_ref[...].astype(jnp.bfloat16).astype(jnp.float32)
    ext_ref[:, hw + n_out:] = hi_ref[...].astype(jnp.float32)
    ext = ext_ref[...]
    for c in range(reach_x):
        xs_ref[c * planes:(c + 1) * planes, :] = lane_shift(ext, c - reach_x // 2, cols).astype(jnp.bfloat16)
    acc = None
    for b in range(reach_y):
        off = (2 * half - b) * cols
        part = jnp.dot(w_ref[b], xs_ref[:, off:off + n_out], preferred_element_type=jnp.float32)
        acc = part if acc is None else acc + part
    for v in range(views):
        rows = slice(v * planes, (v + 1) * planes)
        ratio = (meas_ref[rows, :].astype(jnp.float32) / (acc[rows] + bg_ref[v])).astype(jnp.bfloat16)
        ratio_ref[rows, :] = ratio
        rlo_ref[rows, :] = ratio[:, :hw]
        rhi_ref[rows, :] = ratio[:, n_out - hw:]


def corr_kernel(ratio_ref, lo_ref, hi_ref, base_ref, est_ref, out_ref, ext_ref, w_ref, *,
                cols, reach_y, reach_x, half, half_z, views):
    planes = est_ref.shape[0]
    n_out = est_ref.shape[1]
    hw = half * cols
    lanes = base_ref.shape[2]
    for b in range(reach_y):
        for c in range(reach_x):
            row = base_ref[b, c:c + 1, :].astype(jnp.float32)
            w_ref[b, c * planes:(c + 1) * planes, :] = toeplitz_block(row, planes, half_z, lanes)
    ext_ref[:, :hw] = lo_ref[...]
    ext_ref[:, hw:hw + n_out] = ratio_ref[...]
    ext_ref[:, hw + n_out:] = hi_ref[...]
    acc = None
    for b in range(reach_y):
        off = b * cols
        part = jnp.dot(w_ref[b], ext_ref[:, off:off + n_out], preferred_element_type=jnp.float32)
        acc = part if acc is None else acc + part
    total = None
    for c in range(reach_x):
        piece = lane_shift(acc[c * planes:(c + 1) * planes], reach_x // 2 - c, cols)
        total = piece if total is None else total + piece
    out_ref[...] = est_ref[...] * total / views


def local(measured, start, psf, background):
    planes, rows, cols = start.shape
    views = measured.shape[0]
    reach_y, reach_x = psf.shape[2], psf.shape[3]
    half = reach_y // 2
    half_z = psf.shape[1] // 2
    lanes = -(-(reach_x * planes + half_z) // 128) * 128
    blur_b, corr_b = build_bases(psf, planes, lanes, views * planes)
    n_out = rows * cols
    hw = half * cols
    vmem = pl.BlockSpec(memory_space=pltpu.VMEM)

    start2 = start.reshape(planes, n_out)
    rounded = start2.astype(jnp.bfloat16)
    lo, hi = halos(rounded, "gy", hw)
    meas2 = measured.reshape(views * planes, n_out)
    smem = pl.BlockSpec(memory_space=pltpu.SMEM)

    ratio, rlo, rhi = pl.pallas_call(
        lambda *refs: blur_kernel(*refs, cols=cols, reach_y=reach_y, reach_x=reach_x, half=half, half_z=half_z),
        out_shape=(
            jax.ShapeDtypeStruct((views * planes, n_out), jnp.bfloat16),
            jax.ShapeDtypeStruct((views * planes, hw), jnp.bfloat16),
            jax.ShapeDtypeStruct((views * planes, hw), jnp.bfloat16),
        ),
        in_specs=[vmem] * 5 + [smem],
        out_specs=(vmem, vmem, vmem),
        scratch_shapes=[
            pltpu.VMEM((planes, n_out + 2 * hw), jnp.float32),
            pltpu.VMEM((lanes, n_out + 2 * hw), jnp.bfloat16),
            pltpu.VMEM((reach_y, views * planes, lanes), jnp.bfloat16),
        ],
    )(start2, lo, hi, blur_b, meas2, background)

    before = lax.ppermute(rhi, "gy", [(i, i + 1) for i in range(lax.axis_size("gy") - 1)])
    after = lax.ppermute(rlo, "gy", [(i + 1, i) for i in range(lax.axis_size("gy") - 1)])

    est = pl.pallas_call(
        lambda *refs: corr_kernel(*refs, cols=cols, reach_y=reach_y, reach_x=reach_x, half=half, half_z=half_z,
                                  views=views),
        out_shape=jax.ShapeDtypeStruct((planes, n_out), jnp.float32),
        in_specs=[vmem] * 5,
        out_specs=vmem,
        scratch_shapes=[
            pltpu.VMEM((views * planes, n_out + 2 * hw), jnp.bfloat16),
            pltpu.VMEM((reach_y, reach_x * planes, views * planes), jnp.bfloat16),
        ],
    )(ratio, before, after, corr_b, start2)
    return est.reshape(planes, rows, cols)


def solution(mesh):
    in_specs = (P(None, None, ("parts", "gy"), None), P(None, ("parts", "gy"), None), P(), P())
    out_specs = P(None, ("parts", "gy"), None)
    return jax.shard_map(local, mesh=mesh, in_specs=in_specs, out_specs=out_specs, check_vma=False)
```

```python
import jax
import jax.numpy as jnp
from jax import lax
from jax.experimental import pallas as pl
from jax.experimental.pallas import tpu as pltpu
from jax.sharding import PartitionSpec as P


def build_bases(psf, planes, lanes, corr_lanes):
    kernel = psf / jnp.sum(psf, axis=(1, 2, 3), keepdims=True)
    views, depth, reach_y, reach_x = psf.shape
    half_z = depth // 2
    lane = jnp.arange(lanes, dtype=jnp.int32)
    tap = jnp.arange(depth, dtype=jnp.int32)
    col = jnp.arange(reach_x, dtype=jnp.int32)
    at = (col[None, :, None] * planes + half_z - tap[:, None, None]) % lanes
    onehot = (lane[None, None, :] == at).astype(jnp.float32)
    blur = jnp.einsum("vabc,acl->bvl", kernel, onehot, precision=lax.Precision.HIGHEST)
    view = jnp.arange(views, dtype=jnp.int32)
    at = (view[:, None, None] * planes + tap[None, :, None] - half_z) % corr_lanes
    onehot = (jnp.arange(corr_lanes, dtype=jnp.int32)[None, None, :] == at).astype(jnp.float32)
    corr = jnp.einsum("vabc,val->bcl", kernel, onehot, precision=lax.Precision.HIGHEST)
    return blur.astype(jnp.bfloat16), corr.astype(jnp.bfloat16)


def toeplitz_block(row, planes, half_z, width):
    lanes = row.shape[-1]
    blk = jnp.broadcast_to(row, (planes, lanes))
    blk = pltpu.roll(blk, 0, 1, stride=1, stride_axis=0)
    q = lax.broadcasted_iota(jnp.int32, (planes, lanes), 0)
    l = lax.broadcasted_iota(jnp.int32, (planes, lanes), 1)
    d = l % planes - q
    keep = (d <= half_z) & (d >= -half_z) & (l < width)
    return jnp.where(keep, blk, 0.0).astype(jnp.bfloat16)


def lane_shift(x, shift, cols):
    n = x.shape[-1]
    rolled = pltpu.roll(x, shift % n, x.ndim - 1) if shift % n else x
    col = lax.broadcasted_iota(jnp.int32, x.shape, x.ndim - 1) % cols
    keep = (col - shift >= 0) & (col - shift < cols)
    return jnp.where(keep, rolled, jnp.zeros_like(rolled))


def rl_kernel(start_ref, before_ref, after_ref, bbase_ref, cbase_ref, meas_ref, bg_ref, out_ref,
              ext_ref, xs_ref, wb_ref, wc_ref, mext_ref, rext_ref, *, cols, reach_y, reach_x, half, half_z):
    planes = start_ref.shape[0]
    n_out = start_ref.shape[1]
    views = bbase_ref.shape[1]
    hw = half * cols
    n_mid = n_out + 2 * hw
    width = reach_x * planes
    for b in range(reach_y):
        for v in range(views):
            row = bbase_ref[b, v:v + 1, :].astype(jnp.float32)
            wb_ref[b, v * planes:(v + 1) * planes, :] = toeplitz_block(row, planes, half_z, width)
        for c in range(reach_x):
            row = cbase_ref[b, c:c + 1, :].astype(jnp.float32)
            wc_ref[b, c * planes:(c + 1) * planes, :] = toeplitz_block(row, planes, half_z, views * planes)
    ext_ref[:, :hw] = before_ref[:planes, :].astype(jnp.float32)
    ext_ref[:, hw:2 * hw] = before_ref[planes:2 * planes, :].astype(jnp.float32)
    ext_ref[:, 2 * hw:2 * hw + n_out] = start_ref[...].astype(jnp.bfloat16).astype(jnp.float32)
    ext_ref[:, 2 * hw + n_out:3 * hw + n_out] = after_ref[:planes, :].astype(jnp.float32)
    ext_ref[:, 3 * hw + n_out:] = after_ref[planes:2 * planes, :].astype(jnp.float32)
    mext_ref[:, :hw] = before_ref[2 * planes:, :]
    mext_ref[:, hw:hw + n_out] = meas_ref[...]
    mext_ref[:, hw + n_out:] = after_ref[2 * planes:, :]
    xs_ref[width:, :] = jnp.zeros((xs_ref.shape[0] - width, xs_ref.shape[1]), jnp.bfloat16)
    ext = ext_ref[...]
    for c in range(reach_x):
        xs_ref[c * planes:(c + 1) * planes, :] = lane_shift(ext, c - reach_x // 2, cols).astype(jnp.bfloat16)
    acc = None
    for b in range(reach_y):
        off = (2 * half - b) * cols
        part = jnp.dot(wb_ref[b], xs_ref[:, off:off + n_mid], preferred_element_type=jnp.float32)
        acc = part if acc is None else acc + part
    for v in range(views):
        rows = slice(v * planes, (v + 1) * planes)
        rext_ref[rows, :] = (mext_ref[rows, :].astype(jnp.float32) / (acc[rows] + bg_ref[v])).astype(jnp.bfloat16)
    acc = None
    for b in range(reach_y):
        off = b * cols
        part = jnp.dot(wc_ref[b], rext_ref[:, off:off + n_out], preferred_element_type=jnp.float32)
        acc = part if acc is None else acc + part
    total = None
    for c in range(reach_x):
        piece = lane_shift(acc[c * planes:(c + 1) * planes], reach_x // 2 - c, cols)
        total = piece if total is None else total + piece
    out_ref[...] = start_ref[...] * total / views


def local(measured, start, psf, background):
    planes, rows, cols = start.shape
    views = measured.shape[0]
    reach_y, reach_x = psf.shape[2], psf.shape[3]
    half = reach_y // 2
    half_z = psf.shape[1] // 2
    assert rows >= 2 * half
    lanes = -(-(reach_x * planes + half_z) // 128) * 128
    blur_b, corr_b = build_bases(psf, planes, lanes, views * planes)
    n_out = rows * cols
    hw = half * cols
    vmem = pl.BlockSpec(memory_space=pltpu.VMEM)
    smem = pl.BlockSpec(memory_space=pltpu.SMEM)

    start2 = start.reshape(planes, n_out)
    rounded = start2.astype(jnp.bfloat16)
    meas2 = measured.reshape(views * planes, n_out)
    last = jnp.concatenate(
        [rounded[:, n_out - 2 * hw:n_out - hw], rounded[:, n_out - hw:], meas2[:, n_out - hw:]], axis=0)
    first = jnp.concatenate([rounded[:, :hw], rounded[:, hw:2 * hw], meas2[:, :hw]], axis=0)
    peers = lax.axis_size("gy")
    before = lax.ppermute(last, "gy", [(i, i + 1) for i in range(peers - 1)])
    after = lax.ppermute(first, "gy", [(i + 1, i) for i in range(peers - 1)])

    n_mid = n_out + 2 * hw
    est = pl.pallas_call(
        lambda *refs: rl_kernel(*refs, cols=cols, reach_y=reach_y, reach_x=reach_x, half=half, half_z=half_z),
        out_shape=jax.ShapeDtypeStruct((planes, n_out), jnp.float32),
        in_specs=[vmem] * 6 + [smem],
        out_specs=vmem,
        scratch_shapes=[
            pltpu.VMEM((planes, n_out + 4 * hw), jnp.float32),
            pltpu.VMEM((lanes, n_out + 4 * hw), jnp.bfloat16),
            pltpu.VMEM((reach_y, views * planes, lanes), jnp.bfloat16),
            pltpu.VMEM((reach_y, reach_x * planes, views * planes), jnp.bfloat16),
            pltpu.VMEM((views * planes, n_mid), jnp.bfloat16),
            pltpu.VMEM((views * planes, n_mid), jnp.bfloat16),
        ],
    )(start2, before, after, blur_b, corr_b, meas2, background)
    return est.reshape(planes, rows, cols)


def solution(mesh):
    in_specs = (P(None, None, ("parts", "gy"), None), P(None, ("parts", "gy"), None), P(), P())
    out_specs = P(None, ("parts", "gy"), None)
    return jax.shard_map(local, mesh=mesh, in_specs=in_specs, out_specs=out_specs, check_vma=False)
```

```python
import jax
import jax.numpy as jnp
from jax import lax
from jax.experimental import pallas as pl
from jax.experimental.pallas import tpu as pltpu
from jax.sharding import PartitionSpec as P


def build_bases(psf, planes, lanes, corr_lanes):
    kernel = psf / jnp.sum(psf, axis=(1, 2, 3), keepdims=True)
    views, depth, reach_y, reach_x = psf.shape
    half_z = depth // 2
    lane = jnp.arange(lanes, dtype=jnp.int32)
    tap = jnp.arange(depth, dtype=jnp.int32)
    col = jnp.arange(reach_x, dtype=jnp.int32)
    at = (col[None, :, None] * planes + half_z - tap[:, None, None]) % lanes
    onehot = (lane[None, None, :] == at).astype(jnp.float32)
    blur = jnp.einsum("vabc,acl->bvl", kernel, onehot, precision=lax.Precision.HIGHEST)
    view = jnp.arange(views, dtype=jnp.int32)
    at = (view[:, None, None] * planes + tap[None, :, None] - half_z) % corr_lanes
    onehot = (jnp.arange(corr_lanes, dtype=jnp.int32)[None, None, :] == at).astype(jnp.float32)
    corr = jnp.einsum("vabc,val->bcl", kernel, onehot, precision=lax.Precision.HIGHEST)
    return blur.astype(jnp.bfloat16), corr.astype(jnp.bfloat16)


def toeplitz_block(row, planes, half_z, width):
    lanes = row.shape[-1]
    blk = jnp.broadcast_to(row, (planes, lanes))
    blk = pltpu.roll(blk, 0, 1, stride=1, stride_axis=0)
    q = lax.broadcasted_iota(jnp.int32, (planes, lanes), 0)
    l = lax.broadcasted_iota(jnp.int32, (planes, lanes), 1)
    d = l % planes - q
    keep = (d <= half_z) & (d >= -half_z) & (l < width)
    return jnp.where(keep, blk, 0.0).astype(jnp.bfloat16)


def lane_shift(x, shift, cols):
    n = x.shape[-1]
    rolled = pltpu.roll(x, shift % n, x.ndim - 1) if shift % n else x
    col = lax.broadcasted_iota(jnp.int32, x.shape, x.ndim - 1) % cols
    keep = (col - shift >= 0) & (col - shift < cols)
    return jnp.where(keep, rolled, jnp.zeros_like(rolled))


def rl_kernel(start_ref, before_ref, after_ref, bbase_ref, cbase_ref, meas_ref, bg_ref, out_ref,
              ext_ref, xs_ref, wb_ref, wc_ref, mext_ref, rext_ref, *, cols, reach_y, reach_x, half, half_z):
    planes = start_ref.shape[0]
    n_out = start_ref.shape[1] * cols
    views = bbase_ref.shape[1]
    hw = half * cols
    n_mid = n_out + 2 * hw
    width = reach_x * planes
    for b in range(reach_y):
        for v in range(views):
            row = bbase_ref[b, v:v + 1, :].astype(jnp.float32)
            wb_ref[b, v * planes:(v + 1) * planes, :] = toeplitz_block(row, planes, half_z, width)
        for c in range(reach_x):
            row = cbase_ref[b, c:c + 1, :].astype(jnp.float32)
            wc_ref[b, c * planes:(c + 1) * planes, :] = toeplitz_block(row, planes, half_z, views * planes)
    rows = start_ref.shape[1]
    for j in range(2 * half):
        ext_ref[:, j * cols:(j + 1) * cols] = before_ref[j * planes:(j + 1) * planes, :].astype(jnp.float32)
        at = (2 * half + rows + j) * cols
        ext_ref[:, at:at + cols] = after_ref[j * planes:(j + 1) * planes, :].astype(jnp.float32)
    for r in range(rows):
        at = (2 * half + r) * cols
        ext_ref[:, at:at + cols] = start_ref[:, r, :].astype(jnp.bfloat16).astype(jnp.float32)
    m0 = 2 * half * planes
    vp = views * planes
    for j in range(half):
        mext_ref[:, j * cols:(j + 1) * cols] = before_ref[m0 + j * vp:m0 + (j + 1) * vp, :]
        at = (half + rows + j) * cols
        mext_ref[:, at:at + cols] = after_ref[m0 + j * vp:m0 + (j + 1) * vp, :]
    mext_ref[:, hw:hw + n_out] = meas_ref[...]
    xs_ref[width:, :] = jnp.zeros((xs_ref.shape[0] - width, xs_ref.shape[1]), jnp.bfloat16)
    ext = ext_ref[...]
    for c in range(reach_x):
        xs_ref[c * planes:(c + 1) * planes, :] = lane_shift(ext, c - reach_x // 2, cols).astype(jnp.bfloat16)
    acc = None
    for b in range(reach_y):
        off = (2 * half - b) * cols
        part = jnp.dot(wb_ref[b], xs_ref[:, off:off + n_mid], preferred_element_type=jnp.float32)
        acc = part if acc is None else acc + part
    for v in range(views):
        rows = slice(v * planes, (v + 1) * planes)
        rext_ref[rows, :] = (mext_ref[rows, :].astype(jnp.float32) / (acc[rows] + bg_ref[v])).astype(jnp.bfloat16)
    acc = None
    for b in range(reach_y):
        off = b * cols
        part = jnp.dot(wc_ref[b], rext_ref[:, off:off + n_out], preferred_element_type=jnp.float32)
        acc = part if acc is None else acc + part
    total = None
    for c in range(reach_x):
        piece = lane_shift(acc[c * planes:(c + 1) * planes], reach_x // 2 - c, cols)
        total = piece if total is None else total + piece
    for r in range(start_ref.shape[1]):
        out_ref[:, r, :] = start_ref[:, r, :] * total[:, r * cols:(r + 1) * cols] / views


def local(measured, start, psf, background):
    planes, rows, cols = start.shape
    views = measured.shape[0]
    reach_y, reach_x = psf.shape[2], psf.shape[3]
    half = reach_y // 2
    half_z = psf.shape[1] // 2
    assert rows >= 2 * half
    lanes = -(-(reach_x * planes + half_z) // 128) * 128
    blur_b, corr_b = build_bases(psf, planes, lanes, views * planes)
    n_out = rows * cols
    hw = half * cols
    vmem = pl.BlockSpec(memory_space=pltpu.VMEM)
    smem = pl.BlockSpec(memory_space=pltpu.SMEM)

    rounded = start.astype(jnp.bfloat16)
    meas2 = measured.reshape(views * planes, n_out)

    def slab(lo, hi):
        r = jnp.transpose(rounded[:, lo:hi, :], (1, 0, 2)).reshape(-1, cols)
        return r

    def meas_rows(lo, hi):
        m = jnp.transpose(measured[:, :, lo:hi, :], (2, 0, 1, 3)).reshape(-1, cols)
        return m

    last = jnp.concatenate([slab(rows - 2 * half, rows), meas_rows(rows - half, rows)], axis=0)
    first = jnp.concatenate([slab(0, 2 * half), meas_rows(0, half)], axis=0)
    peers = lax.axis_size("gy")
    before = lax.ppermute(last, "gy", [(i, i + 1) for i in range(peers - 1)])
    after = lax.ppermute(first, "gy", [(i + 1, i) for i in range(peers - 1)])

    n_mid = n_out + 2 * hw
    est = pl.pallas_call(
        lambda *refs: rl_kernel(*refs, cols=cols, reach_y=reach_y, reach_x=reach_x, half=half, half_z=half_z),
        out_shape=jax.ShapeDtypeStruct((planes, rows, cols), jnp.float32),
        in_specs=[vmem] * 6 + [smem],
        out_specs=vmem,
        scratch_shapes=[
            pltpu.VMEM((planes, n_out + 4 * hw), jnp.float32),
            pltpu.VMEM((lanes, n_out + 4 * hw), jnp.bfloat16),
            pltpu.VMEM((reach_y, views * planes, lanes), jnp.bfloat16),
            pltpu.VMEM((reach_y, reach_x * planes, views * planes), jnp.bfloat16),
            pltpu.VMEM((views * planes, n_mid), jnp.bfloat16),
            pltpu.VMEM((views * planes, n_mid), jnp.bfloat16),
        ],
    )(start, before, after, blur_b, corr_b, meas2, background)
    return est


def solution(mesh):
    in_specs = (P(None, None, ("parts", "gy"), None), P(None, ("parts", "gy"), None), P(), P())
    out_specs = P(None, ("parts", "gy"), None)
    return jax.shard_map(local, mesh=mesh, in_specs=in_specs, out_specs=out_specs, check_vma=False)
```

```python
import jax
import jax.numpy as jnp
from jax import lax
from jax.experimental import pallas as pl
from jax.experimental.pallas import tpu as pltpu
from jax.sharding import PartitionSpec as P


def build_bases(psf, planes, lanes, corr_lanes):
    kernel = psf / jnp.sum(psf, axis=(1, 2, 3), keepdims=True)
    views, depth, reach_y, reach_x = psf.shape
    half_z = depth // 2
    lane = jnp.arange(lanes, dtype=jnp.int32)
    tap = jnp.arange(depth, dtype=jnp.int32)
    col = jnp.arange(reach_x, dtype=jnp.int32)
    at = (col[None, :, None] * planes + half_z - tap[:, None, None]) % lanes
    onehot = (lane[None, None, :] == at).astype(jnp.float32)
    blur = jnp.einsum("vabc,acl->bvl", kernel, onehot, precision=lax.Precision.HIGHEST)
    view = jnp.arange(views, dtype=jnp.int32)
    at = (view[:, None, None] * planes + tap[None, :, None] - half_z) % corr_lanes
    onehot = (jnp.arange(corr_lanes, dtype=jnp.int32)[None, None, :] == at).astype(jnp.float32)
    corr = jnp.einsum("vabc,val->bcl", kernel, onehot, precision=lax.Precision.HIGHEST)
    return blur.astype(jnp.bfloat16), corr.astype(jnp.bfloat16)


def toeplitz_block(row, planes, half_z, width):
    lanes = row.shape[-1]
    blk = jnp.broadcast_to(row, (planes, lanes))
    blk = pltpu.roll(blk, 0, 1, stride=1, stride_axis=0)
    q = lax.broadcasted_iota(jnp.int32, (planes, lanes), 0)
    l = lax.broadcasted_iota(jnp.int32, (planes, lanes), 1)
    d = l % planes - q
    keep = (d <= half_z) & (d >= -half_z) & (l < width)
    return jnp.where(keep, blk, 0.0).astype(jnp.bfloat16)


def lane_shift(x, shift, cols):
    n = x.shape[-1]
    rolled = pltpu.roll(x, shift % n, x.ndim - 1) if shift % n else x
    col = lax.broadcasted_iota(jnp.int32, x.shape, x.ndim - 1) % cols
    keep = (col - shift >= 0) & (col - shift < cols)
    return jnp.where(keep, rolled, jnp.zeros_like(rolled))


def weights_kernel(bbase_ref, cbase_ref, wb_ref, wc_ref, *, planes, half_z, width):
    reach_y, views = bbase_ref.shape[0], bbase_ref.shape[1]
    reach_x = cbase_ref.shape[1]
    for b in range(reach_y):
        for v in range(views):
            row = bbase_ref[b, v:v + 1, :].astype(jnp.float32)
            wb_ref[b, v * planes:(v + 1) * planes, :] = toeplitz_block(row, planes, half_z, width)
        for c in range(reach_x):
            row = cbase_ref[b, c:c + 1, :].astype(jnp.float32)
            wc_ref[b, c * planes:(c + 1) * planes, :] = toeplitz_block(row, planes, half_z, views * planes)


def rl_kernel(start_ref, before_ref, after_ref, wb_hbm, wc_hbm, meas_ref, bg_ref, out_ref,
              ext_ref, xs_ref, wb_ref, wc_ref, mext_ref, rext_ref, sems, *, cols, reach_y, reach_x, half, half_z):
    planes = start_ref.shape[0]
    n_out = start_ref.shape[1] * cols
    views = meas_ref.shape[0] // planes
    hw = half * cols
    n_mid = n_out + 2 * hw
    width = reach_x * planes
    copy_b = pltpu.make_async_copy(wb_hbm, wb_ref, sems.at[0])
    copy_c = pltpu.make_async_copy(wc_hbm, wc_ref, sems.at[1])
    copy_b.start()
    copy_c.start()
    rows = start_ref.shape[1]
    for j in range(2 * half):
        ext_ref[:, j * cols:(j + 1) * cols] = before_ref[j * planes:(j + 1) * planes, :].astype(jnp.float32)
        at = (2 * half + rows + j) * cols
        ext_ref[:, at:at + cols] = after_ref[j * planes:(j + 1) * planes, :].astype(jnp.float32)
    for r in range(rows):
        at = (2 * half + r) * cols
        ext_ref[:, at:at + cols] = start_ref[:, r, :].astype(jnp.bfloat16).astype(jnp.float32)
    m0 = 2 * half * planes
    vp = views * planes
    for j in range(half):
        mext_ref[:, j * cols:(j + 1) * cols] = before_ref[m0 + j * vp:m0 + (j + 1) * vp, :]
        at = (half + rows + j) * cols
        mext_ref[:, at:at + cols] = after_ref[m0 + j * vp:m0 + (j + 1) * vp, :]
    mext_ref[:, hw:hw + n_out] = meas_ref[...]
    xs_ref[width:, :] = jnp.zeros((xs_ref.shape[0] - width, xs_ref.shape[1]), jnp.bfloat16)
    ext = ext_ref[...]
    for c in range(reach_x):
        xs_ref[c * planes:(c + 1) * planes, :] = lane_shift(ext, c - reach_x // 2, cols).astype(jnp.bfloat16)
    copy_b.wait()
    acc = None
    for b in range(reach_y):
        off = (2 * half - b) * cols
        part = jnp.dot(wb_ref[b], xs_ref[:, off:off + n_mid], preferred_element_type=jnp.float32)
        acc = part if acc is None else acc + part
    for v in range(views):
        rows = slice(v * planes, (v + 1) * planes)
        rext_ref[rows, :] = (mext_ref[rows, :].astype(jnp.float32) / (acc[rows] + bg_ref[v])).astype(jnp.bfloat16)
    copy_c.wait()
    acc = None
    for b in range(reach_y):
        off = b * cols
        part = jnp.dot(wc_ref[b], rext_ref[:, off:off + n_out], preferred_element_type=jnp.float32)
        acc = part if acc is None else acc + part
    total = None
    for c in range(reach_x):
        piece = lane_shift(acc[c * planes:(c + 1) * planes], reach_x // 2 - c, cols)
        total = piece if total is None else total + piece
    for r in range(start_ref.shape[1]):
        out_ref[:, r, :] = start_ref[:, r, :] * total[:, r * cols:(r + 1) * cols] / views


def local(measured, start, psf, background):
    planes, rows, cols = start.shape
    views = measured.shape[0]
    reach_y, reach_x = psf.shape[2], psf.shape[3]
    half = reach_y // 2
    half_z = psf.shape[1] // 2
    assert rows >= 2 * half
    lanes = -(-(reach_x * planes + half_z) // 128) * 128
    blur_b, corr_b = build_bases(psf, planes, lanes, views * planes)
    n_out = rows * cols
    hw = half * cols
    vmem = pl.BlockSpec(memory_space=pltpu.VMEM)
    smem = pl.BlockSpec(memory_space=pltpu.SMEM)

    rounded = start.astype(jnp.bfloat16)
    meas2 = measured.reshape(views * planes, n_out)

    def slab(lo, hi):
        r = jnp.transpose(rounded[:, lo:hi, :], (1, 0, 2)).reshape(-1, cols)
        return r

    def meas_rows(lo, hi):
        m = jnp.transpose(measured[:, :, lo:hi, :], (2, 0, 1, 3)).reshape(-1, cols)
        return m

    last = jnp.concatenate([slab(rows - 2 * half, rows), meas_rows(rows - half, rows)], axis=0)
    first = jnp.concatenate([slab(0, 2 * half), meas_rows(0, half)], axis=0)
    peers = lax.axis_size("gy")
    before = lax.ppermute(last, "gy", [(i, i + 1) for i in range(peers - 1)])
    after = lax.ppermute(first, "gy", [(i + 1, i) for i in range(peers - 1)])

    n_mid = n_out + 2 * hw
    wb, wc = pl.pallas_call(
        lambda *refs: weights_kernel(*refs, planes=planes, half_z=half_z, width=reach_x * planes),
        out_shape=(
            jax.ShapeDtypeStruct((reach_y, views * planes, lanes), jnp.bfloat16),
            jax.ShapeDtypeStruct((reach_y, reach_x * planes, views * planes), jnp.bfloat16),
        ),
        in_specs=[vmem] * 2,
        out_specs=(vmem, vmem),
    )(blur_b, corr_b)
    anyspace = pl.BlockSpec(memory_space=pl.ANY)
    est = pl.pallas_call(
        lambda *refs: rl_kernel(*refs, cols=cols, reach_y=reach_y, reach_x=reach_x, half=half, half_z=half_z),
        out_shape=jax.ShapeDtypeStruct((planes, rows, cols), jnp.float32),
        in_specs=[vmem] * 3 + [anyspace] * 2 + [vmem, smem],
        out_specs=vmem,
        scratch_shapes=[
            pltpu.VMEM((planes, n_out + 4 * hw), jnp.float32),
            pltpu.VMEM((lanes, n_out + 4 * hw), jnp.bfloat16),
            pltpu.VMEM((reach_y, views * planes, lanes), jnp.bfloat16),
            pltpu.VMEM((reach_y, reach_x * planes, views * planes), jnp.bfloat16),
            pltpu.VMEM((views * planes, n_mid), jnp.bfloat16),
            pltpu.VMEM((views * planes, n_mid), jnp.bfloat16),
            pltpu.SemaphoreType.DMA((2,)),
        ],
    )(start, before, after, wb, wc, meas2, background)
    return est


def solution(mesh):
    in_specs = (P(None, None, ("parts", "gy"), None), P(None, ("parts", "gy"), None), P(), P())
    out_specs = P(None, ("parts", "gy"), None)
    return jax.shard_map(local, mesh=mesh, in_specs=in_specs, out_specs=out_specs, check_vma=False)
```

```python
import jax
import jax.numpy as jnp
from jax import lax
from jax.experimental import pallas as pl
from jax.experimental.pallas import tpu as pltpu
from jax.sharding import PartitionSpec as P


def build_bases(psf, planes, lanes, corr_lanes):
    kernel = psf / jnp.sum(psf, axis=(1, 2, 3), keepdims=True)
    views, depth, reach_y, reach_x = psf.shape
    half_z = depth // 2
    lane = jnp.arange(lanes, dtype=jnp.int32)
    tap = jnp.arange(depth, dtype=jnp.int32)
    col = jnp.arange(reach_x, dtype=jnp.int32)
    at = (col[None, :, None] * planes + half_z - tap[:, None, None]) % lanes
    onehot = (lane[None, None, :] == at).astype(jnp.float32)
    blur = jnp.einsum("vabc,acl->bvl", kernel, onehot, precision=lax.Precision.HIGHEST)
    view = jnp.arange(views, dtype=jnp.int32)
    at = (view[:, None, None] * planes + tap[None, :, None] - half_z) % corr_lanes
    onehot = (jnp.arange(corr_lanes, dtype=jnp.int32)[None, None, :] == at).astype(jnp.float32)
    corr = jnp.einsum("vabc,val->bcl", kernel, onehot, precision=lax.Precision.HIGHEST)
    return blur.astype(jnp.bfloat16), corr.astype(jnp.bfloat16)


def toeplitz_block(row, planes, half_z, width):
    lanes = row.shape[-1]
    blk = jnp.broadcast_to(row, (planes, lanes))
    blk = pltpu.roll(blk, 0, 1, stride=1, stride_axis=0)
    q = lax.broadcasted_iota(jnp.int32, (planes, lanes), 0)
    l = lax.broadcasted_iota(jnp.int32, (planes, lanes), 1)
    d = l % planes - q
    keep = (d <= half_z) & (d >= -half_z) & (l < width)
    return jnp.where(keep, blk, 0.0).astype(jnp.bfloat16)


def lane_shift(x, shift, cols):
    n = x.shape[-1]
    rolled = pltpu.roll(x, shift % n, x.ndim - 1) if shift % n else x
    col = lax.broadcasted_iota(jnp.int32, x.shape, x.ndim - 1) % cols
    keep = (col - shift >= 0) & (col - shift < cols)
    return jnp.where(keep, rolled, jnp.zeros_like(rolled))


def rl_kernel(start_ref, before_ref, after_ref, bbase_ref, cbase_ref, meas_ref, bg_ref, out_ref,
              xs_ref, wb_ref, wc_ref, rext_ref, *, cols, reach_y, reach_x, half, half_z):
    planes = start_ref.shape[0]
    n_out = start_ref.shape[1] * cols
    views = bbase_ref.shape[1]
    hw = half * cols
    n_mid = n_out + 2 * hw
    width = reach_x * planes
    for b in range(reach_y):
        for v in range(views):
            row = bbase_ref[b, v:v + 1, :].astype(jnp.float32)
            wb_ref[b, v * planes:(v + 1) * planes, :] = toeplitz_block(row, planes, half_z, width)
        for c in range(reach_x):
            row = cbase_ref[b, c:c + 1, :].astype(jnp.float32)
            wc_ref[b, c * planes:(c + 1) * planes, :] = toeplitz_block(row, planes, half_z, views * planes)
    rows = start_ref.shape[1]
    vp = views * planes
    m0 = 2 * half * planes

    def rounded_slab(e):
        if e < 2 * half:
            return before_ref[e * planes:(e + 1) * planes, :].astype(jnp.float32)
        if e >= 2 * half + rows:
            j = e - 2 * half - rows
            return after_ref[j * planes:(j + 1) * planes, :].astype(jnp.float32)
        return start_ref[:, e - 2 * half, :].astype(jnp.bfloat16).astype(jnp.float32)

    def measured_slab(m):
        if m < half:
            return before_ref[m0 + m * vp:m0 + (m + 1) * vp, :]
        if m >= half + rows:
            j = m - half - rows
            return after_ref[m0 + j * vp:m0 + (j + 1) * vp, :]
        return meas_ref[:, (m - half) * cols:(m - half + 1) * cols]

    xs_ref[width:, :] = jnp.zeros((xs_ref.shape[0] - width, xs_ref.shape[1]), jnp.bfloat16)
    for e in range(rows + 4 * half):
        slab = rounded_slab(e)
        for c in range(reach_x):
            xs_ref[c * planes:(c + 1) * planes, e * cols:(e + 1) * cols] = (
                lane_shift(slab, c - reach_x // 2, cols).astype(jnp.bfloat16))
    step = 2 * cols
    for k in range(n_mid // step):
        acc = None
        for b in range(reach_y):
            off = (2 * half - b) * cols + k * step
            part = jnp.dot(wb_ref[b], xs_ref[:, off:off + step], preferred_element_type=jnp.float32)
            acc = part if acc is None else acc + part
        for i in range(step // cols):
            m = k * (step // cols) + i
            meas = measured_slab(m)
            for v in range(views):
                rs = slice(v * planes, (v + 1) * planes)
                ratio = meas[rs].astype(jnp.float32) / (acc[rs, i * cols:(i + 1) * cols] + bg_ref[v])
                rext_ref[rs, m * cols:(m + 1) * cols] = ratio.astype(jnp.bfloat16)
    for k in range(n_out // step):
        acc = None
        for b in range(reach_y):
            off = b * cols + k * step
            part = jnp.dot(wc_ref[b], rext_ref[:, off:off + step], preferred_element_type=jnp.float32)
            acc = part if acc is None else acc + part
        total = None
        for c in range(reach_x):
            piece = lane_shift(acc[c * planes:(c + 1) * planes], reach_x // 2 - c, cols)
            total = piece if total is None else total + piece
        for i in range(step // cols):
            r = k * (step // cols) + i
            out_ref[:, r, :] = start_ref[:, r, :] * total[:, i * cols:(i + 1) * cols] / views


def local(measured, start, psf, background):
    planes, rows, cols = start.shape
    views = measured.shape[0]
    reach_y, reach_x = psf.shape[2], psf.shape[3]
    half = reach_y // 2
    half_z = psf.shape[1] // 2
    assert rows >= 2 * half and rows % 2 == 0
    lanes = -(-(reach_x * planes + half_z) // 128) * 128
    blur_b, corr_b = build_bases(psf, planes, lanes, views * planes)
    n_out = rows * cols
    hw = half * cols
    vmem = pl.BlockSpec(memory_space=pltpu.VMEM)
    smem = pl.BlockSpec(memory_space=pltpu.SMEM)

    rounded = start.astype(jnp.bfloat16)
    meas2 = measured.reshape(views * planes, n_out)

    def slab(lo, hi):
        r = jnp.transpose(rounded[:, lo:hi, :], (1, 0, 2)).reshape(-1, cols)
        return r

    def meas_rows(lo, hi):
        m = jnp.transpose(measured[:, :, lo:hi, :], (2, 0, 1, 3)).reshape(-1, cols)
        return m

    last = jnp.concatenate([slab(rows - 2 * half, rows), meas_rows(rows - half, rows)], axis=0)
    first = jnp.concatenate([slab(0, 2 * half), meas_rows(0, half)], axis=0)
    peers = lax.axis_size("gy")
    before = lax.ppermute(last, "gy", [(i, i + 1) for i in range(peers - 1)])
    after = lax.ppermute(first, "gy", [(i + 1, i) for i in range(peers - 1)])

    n_mid = n_out + 2 * hw
    est = pl.pallas_call(
        lambda *refs: rl_kernel(*refs, cols=cols, reach_y=reach_y, reach_x=reach_x, half=half, half_z=half_z),
        out_shape=jax.ShapeDtypeStruct((planes, rows, cols), jnp.float32),
        in_specs=[vmem] * 6 + [smem],
        out_specs=vmem,
        scratch_shapes=[
            pltpu.VMEM((lanes, n_out + 4 * hw), jnp.bfloat16),
            pltpu.VMEM((reach_y, views * planes, lanes), jnp.bfloat16),
            pltpu.VMEM((reach_y, reach_x * planes, views * planes), jnp.bfloat16),
            pltpu.VMEM((views * planes, n_mid), jnp.bfloat16),
        ],
    )(start, before, after, blur_b, corr_b, meas2, background)
    return est


def solution(mesh):
    in_specs = (P(None, None, ("parts", "gy"), None), P(None, ("parts", "gy"), None), P(), P())
    out_specs = P(None, ("parts", "gy"), None)
    return jax.shard_map(local, mesh=mesh, in_specs=in_specs, out_specs=out_specs, check_vma=False)
```

```python
import jax
import jax.numpy as jnp
from jax import lax
from jax.experimental import pallas as pl
from jax.experimental.pallas import tpu as pltpu
from jax.sharding import PartitionSpec as P


def build_bases(psf, planes, lanes, corr_lanes):
    kernel = psf / jnp.sum(psf, axis=(1, 2, 3), keepdims=True)
    views, depth, reach_y, reach_x = psf.shape
    half_z = depth // 2
    lane = jnp.arange(lanes, dtype=jnp.int32)
    tap = jnp.arange(depth, dtype=jnp.int32)
    col = jnp.arange(reach_x, dtype=jnp.int32)
    at = (col[None, :, None] * planes + half_z - tap[:, None, None]) % lanes
    onehot = (lane[None, None, :] == at).astype(jnp.float32)
    blur = jnp.einsum("vabc,acl->bvl", kernel, onehot, precision=lax.Precision.HIGHEST)
    view = jnp.arange(views, dtype=jnp.int32)
    at = (view[:, None, None] * planes + tap[None, :, None] - half_z) % corr_lanes
    onehot = (jnp.arange(corr_lanes, dtype=jnp.int32)[None, None, :] == at).astype(jnp.float32)
    corr = jnp.einsum("vabc,val->bcl", kernel, onehot, precision=lax.Precision.HIGHEST)
    return blur.astype(jnp.bfloat16), corr.astype(jnp.bfloat16)


def toeplitz_block(row, planes, half_z, width):
    lanes = row.shape[-1]
    blk = jnp.broadcast_to(row, (planes, lanes))
    blk = pltpu.roll(blk, 0, 1, stride=1, stride_axis=0)
    q = lax.broadcasted_iota(jnp.int32, (planes, lanes), 0)
    l = lax.broadcasted_iota(jnp.int32, (planes, lanes), 1)
    d = l % planes - q
    keep = (d <= half_z) & (d >= -half_z) & (l < width)
    return jnp.where(keep, blk, 0.0).astype(jnp.bfloat16)


def lane_shift(x, shift, cols):
    n = x.shape[-1]
    rolled = pltpu.roll(x, shift % n, x.ndim - 1) if shift % n else x
    col = lax.broadcasted_iota(jnp.int32, x.shape, x.ndim - 1) % cols
    keep = (col - shift >= 0) & (col - shift < cols)
    return jnp.where(keep, rolled, jnp.zeros_like(rolled))


def prep_kernel(start_ref, meas_ref, last_ref, first_ref, meas2_ref, *, half):
    planes, rows, cols = start_ref.shape
    vp = meas_ref.shape[0]
    m0 = 2 * half * planes
    for r in range(rows):
        slab = meas_ref[:, r, :]
        meas2_ref[:, r * cols:(r + 1) * cols] = slab
        rounded = start_ref[:, r, :].astype(jnp.bfloat16)
        if r < half:
            first_ref[m0 + r * vp:m0 + (r + 1) * vp, :] = slab
        if r >= rows - half:
            j = r - (rows - half)
            last_ref[m0 + j * vp:m0 + (j + 1) * vp, :] = slab
        if r < 2 * half:
            first_ref[r * planes:(r + 1) * planes, :] = rounded
        if r >= rows - 2 * half:
            j = r - (rows - 2 * half)
            last_ref[j * planes:(j + 1) * planes, :] = rounded


def rl_kernel(start_ref, before_ref, after_ref, bbase_ref, cbase_ref, meas_ref, bg_ref, out_ref,
              xs_ref, wb_ref, wc_ref, rext_ref, *, cols, reach_y, reach_x, half, half_z):
    planes = start_ref.shape[0]
    n_out = start_ref.shape[1] * cols
    views = bbase_ref.shape[1]
    hw = half * cols
    n_mid = n_out + 2 * hw
    width = reach_x * planes
    for b in range(reach_y):
        for v in range(views):
            row = bbase_ref[b, v:v + 1, :].astype(jnp.float32)
            wb_ref[b, v * planes:(v + 1) * planes, :] = toeplitz_block(row, planes, half_z, width)
        for c in range(reach_x):
            row = cbase_ref[b, c:c + 1, :].astype(jnp.float32)
            wc_ref[b, c * planes:(c + 1) * planes, :] = toeplitz_block(row, planes, half_z, views * planes)
    rows = start_ref.shape[1]
    vp = views * planes
    m0 = 2 * half * planes

    def rounded_slab(e):
        if e < 2 * half:
            return before_ref[e * planes:(e + 1) * planes, :].astype(jnp.float32)
        if e >= 2 * half + rows:
            j = e - 2 * half - rows
            return after_ref[j * planes:(j + 1) * planes, :].astype(jnp.float32)
        return start_ref[:, e - 2 * half, :].astype(jnp.bfloat16).astype(jnp.float32)

    def measured_slab(m):
        if m < half:
            return before_ref[m0 + m * vp:m0 + (m + 1) * vp, :]
        if m >= half + rows:
            j = m - half - rows
            return after_ref[m0 + j * vp:m0 + (j + 1) * vp, :]
        return meas_ref[:, (m - half) * cols:(m - half + 1) * cols]

    xs_ref[width:, :] = jnp.zeros((xs_ref.shape[0] - width, xs_ref.shape[1]), jnp.bfloat16)
    for e in range(rows + 4 * half):
        slab = rounded_slab(e)
        for c in range(reach_x):
            xs_ref[c * planes:(c + 1) * planes, e * cols:(e + 1) * cols] = (
                lane_shift(slab, c - reach_x // 2, cols).astype(jnp.bfloat16))
    step = 2 * cols
    for k in range(n_mid // step):
        acc = None
        for b in range(reach_y):
            off = (2 * half - b) * cols + k * step
            part = jnp.dot(wb_ref[b], xs_ref[:, off:off + step], preferred_element_type=jnp.float32)
            acc = part if acc is None else acc + part
        for i in range(step // cols):
            m = k * (step // cols) + i
            meas = measured_slab(m)
            for v in range(views):
                rs = slice(v * planes, (v + 1) * planes)
                ratio = meas[rs].astype(jnp.float32) / (acc[rs, i * cols:(i + 1) * cols] + bg_ref[v])
                rext_ref[rs, m * cols:(m + 1) * cols] = ratio.astype(jnp.bfloat16)
    for k in range(n_out // step):
        acc = None
        for b in range(reach_y):
            off = b * cols + k * step
            part = jnp.dot(wc_ref[b], rext_ref[:, off:off + step], preferred_element_type=jnp.float32)
            acc = part if acc is None else acc + part
        total = None
        for c in range(reach_x):
            piece = lane_shift(acc[c * planes:(c + 1) * planes], reach_x // 2 - c, cols)
            total = piece if total is None else total + piece
        for i in range(step // cols):
            r = k * (step // cols) + i
            out_ref[:, r, :] = start_ref[:, r, :] * total[:, i * cols:(i + 1) * cols] / views


def local(measured, start, psf, background):
    planes, rows, cols = start.shape
    views = measured.shape[0]
    reach_y, reach_x = psf.shape[2], psf.shape[3]
    half = reach_y // 2
    half_z = psf.shape[1] // 2
    assert rows >= 2 * half and rows % 2 == 0
    lanes = -(-(reach_x * planes + half_z) // 128) * 128
    blur_b, corr_b = build_bases(psf, planes, lanes, views * planes)
    n_out = rows * cols
    hw = half * cols
    vmem = pl.BlockSpec(memory_space=pltpu.VMEM)
    smem = pl.BlockSpec(memory_space=pltpu.SMEM)

    n_slab = 2 * half * planes + half * views * planes
    last, first, meas2 = pl.pallas_call(
        lambda *refs: prep_kernel(*refs, half=half),
        out_shape=(
            jax.ShapeDtypeStruct((n_slab, cols), jnp.bfloat16),
            jax.ShapeDtypeStruct((n_slab, cols), jnp.bfloat16),
            jax.ShapeDtypeStruct((views * planes, n_out), jnp.bfloat16),
        ),
        in_specs=[vmem] * 2,
        out_specs=(vmem, vmem, vmem),
    )(start, measured.reshape(views * planes, rows, cols))
    peers = lax.axis_size("gy")
    before = lax.ppermute(last, "gy", [(i, i + 1) for i in range(peers - 1)])
    after = lax.ppermute(first, "gy", [(i + 1, i) for i in range(peers - 1)])

    n_mid = n_out + 2 * hw
    est = pl.pallas_call(
        lambda *refs: rl_kernel(*refs, cols=cols, reach_y=reach_y, reach_x=reach_x, half=half, half_z=half_z),
        out_shape=jax.ShapeDtypeStruct((planes, rows, cols), jnp.float32),
        in_specs=[vmem] * 6 + [smem],
        out_specs=vmem,
        scratch_shapes=[
            pltpu.VMEM((lanes, n_out + 4 * hw), jnp.bfloat16),
            pltpu.VMEM((reach_y, views * planes, lanes), jnp.bfloat16),
            pltpu.VMEM((reach_y, reach_x * planes, views * planes), jnp.bfloat16),
            pltpu.VMEM((views * planes, n_mid), jnp.bfloat16),
        ],
    )(start, before, after, blur_b, corr_b, meas2, background)
    return est


def solution(mesh):
    in_specs = (P(None, None, ("parts", "gy"), None), P(None, ("parts", "gy"), None), P(), P())
    out_specs = P(None, ("parts", "gy"), None)
    return jax.shard_map(local, mesh=mesh, in_specs=in_specs, out_specs=out_specs, check_vma=False)
```

```python
import jax
import jax.numpy as jnp
from jax import lax
from jax.experimental import pallas as pl
from jax.experimental.pallas import tpu as pltpu
from jax.sharding import PartitionSpec as P


def build_bases(psf, planes, lanes, corr_lanes):
    kernel = psf / jnp.sum(psf, axis=(1, 2, 3), keepdims=True)
    views, depth, reach_y, reach_x = psf.shape
    half_z = depth // 2
    lane = jnp.arange(lanes, dtype=jnp.int32)
    tap = jnp.arange(depth, dtype=jnp.int32)
    col = jnp.arange(reach_x, dtype=jnp.int32)
    at = (col[None, :, None] * planes + half_z - tap[:, None, None]) % lanes
    onehot = (lane[None, None, :] == at).astype(jnp.float32)
    blur = jnp.einsum("vabc,acl->bvl", kernel, onehot, precision=lax.Precision.HIGHEST)
    view = jnp.arange(views, dtype=jnp.int32)
    at = (view[:, None, None] * planes + tap[None, :, None] - half_z) % corr_lanes
    onehot = (jnp.arange(corr_lanes, dtype=jnp.int32)[None, None, :] == at).astype(jnp.float32)
    corr = jnp.einsum("vabc,val->bcl", kernel, onehot, precision=lax.Precision.HIGHEST)
    return blur.astype(jnp.bfloat16), corr.astype(jnp.bfloat16)


def toeplitz_block(row, planes, half_z, width):
    lanes = row.shape[-1]
    blk = jnp.broadcast_to(row, (planes, lanes))
    blk = pltpu.roll(blk, 0, 1, stride=1, stride_axis=0)
    q = lax.broadcasted_iota(jnp.int32, (planes, lanes), 0)
    l = lax.broadcasted_iota(jnp.int32, (planes, lanes), 1)
    d = l % planes - q
    keep = (d <= half_z) & (d >= -half_z) & (l < width)
    return jnp.where(keep, blk, 0.0).astype(jnp.bfloat16)


def lane_shift(x, shift, cols):
    n = x.shape[-1]
    rolled = pltpu.roll(x, shift % n, x.ndim - 1) if shift % n else x
    col = lax.broadcasted_iota(jnp.int32, x.shape, x.ndim - 1) % cols
    keep = (col - shift >= 0) & (col - shift < cols)
    return jnp.where(keep, rolled, jnp.zeros_like(rolled))


def rl_kernel(start_ref, before_ref, after_ref, bbase_ref, cbase_ref, meas_ref, bg_ref,
              tot_ref, up_ref, down_ref, xs_ref, wb_ref, wc_ref, rext_ref, *, cols, reach_y, reach_x, half, half_z):
    planes, rows = start_ref.shape[0], start_ref.shape[1]
    views = bbase_ref.shape[1]
    width = reach_x * planes
    for b in range(reach_y):
        for v in range(views):
            row = bbase_ref[b, v:v + 1, :].astype(jnp.float32)
            wb_ref[b, v * planes:(v + 1) * planes, :] = toeplitz_block(row, planes, half_z, width)
        for c in range(reach_x):
            row = cbase_ref[b, c:c + 1, :].astype(jnp.float32)
            wc_ref[b, c * planes:(c + 1) * planes, :] = toeplitz_block(row, planes, half_z, views * planes)

    def rounded_slab(e):
        if e < half:
            return before_ref[e * planes:(e + 1) * planes, :].astype(jnp.float32)
        if e >= half + rows:
            j = e - half - rows
            return after_ref[j * planes:(j + 1) * planes, :].astype(jnp.float32)
        return start_ref[:, e - half, :].astype(jnp.bfloat16).astype(jnp.float32)

    xs_ref[width:, :] = jnp.zeros((xs_ref.shape[0] - width, xs_ref.shape[1]), jnp.bfloat16)
    for e in range(rows + 2 * half):
        slab = rounded_slab(e)
        for c in range(reach_x):
            xs_ref[c * planes:(c + 1) * planes, e * cols:(e + 1) * cols] = (
                lane_shift(slab, c - reach_x // 2, cols).astype(jnp.bfloat16))
    pad = 2 * half * cols
    zeros = jnp.zeros((rext_ref.shape[0], pad), jnp.bfloat16)
    rext_ref[:, :pad] = zeros
    rext_ref[:, pad + rows * cols:] = zeros
    step = 2 * cols
    for k in range(rows * cols // step):
        acc = None
        for b in range(reach_y):
            off = (2 * half - b) * cols + k * step
            part = jnp.dot(wb_ref[b], xs_ref[:, off:off + step], preferred_element_type=jnp.float32)
            acc = part if acc is None else acc + part
        for v in range(views):
            rs = slice(v * planes, (v + 1) * planes)
            ratio = meas_ref[rs, k * step:(k + 1) * step].astype(jnp.float32) / (acc[rs] + bg_ref[v])
            rext_ref[rs, pad + k * step:pad + (k + 1) * step] = ratio.astype(jnp.bfloat16)
    for k in range((rows + 2 * half) * cols // step):
        acc = None
        for b in range(reach_y):
            off = b * cols + k * step
            part = jnp.dot(wc_ref[b], rext_ref[:, off:off + step], preferred_element_type=jnp.float32)
            acc = part if acc is None else acc + part
        total = None
        for c in range(reach_x):
            piece = lane_shift(acc[c * planes:(c + 1) * planes], reach_x // 2 - c, cols)
            total = piece if total is None else total + piece
        for i in range(step // cols):
            o = k * (step // cols) + i - half
            t = total[:, i * cols:(i + 1) * cols]
            if o < 0:
                up_ref[(o + half) * planes:(o + half + 1) * planes, :] = t
            elif o >= rows:
                down_ref[(o - rows) * planes:(o - rows + 1) * planes, :] = t
            else:
                tot_ref[:, o, :] = t


def local(measured, start, psf, background):
    planes, rows, cols = start.shape
    views = measured.shape[0]
    reach_y, reach_x = psf.shape[2], psf.shape[3]
    half = reach_y // 2
    half_z = psf.shape[1] // 2
    assert rows >= half and rows % 2 == 0
    lanes = -(-(reach_x * planes + half_z) // 128) * 128
    blur_b, corr_b = build_bases(psf, planes, lanes, views * planes)
    n_out = rows * cols
    vmem = pl.BlockSpec(memory_space=pltpu.VMEM)
    smem = pl.BlockSpec(memory_space=pltpu.SMEM)
    meas2 = measured.reshape(views * planes, n_out)
    peers = lax.axis_size("gy")
    up = [(i, i + 1) for i in range(peers - 1)]
    down = [(i + 1, i) for i in range(peers - 1)]

    def slab(x, lo, hi):
        return jnp.transpose(x[:, lo:hi, :], (1, 0, 2)).reshape(-1, cols)

    rounded = start.astype(jnp.bfloat16)
    before = lax.ppermute(slab(rounded, rows - half, rows), "gy", up)
    after = lax.ppermute(slab(rounded, 0, half), "gy", down)

    tot, to_up, to_down = pl.pallas_call(
        lambda *refs: rl_kernel(*refs, cols=cols, reach_y=reach_y, reach_x=reach_x, half=half, half_z=half_z),
        out_shape=(
            jax.ShapeDtypeStruct((planes, rows, cols), jnp.float32),
            jax.ShapeDtypeStruct((half * planes, cols), jnp.float32),
            jax.ShapeDtypeStruct((half * planes, cols), jnp.float32),
        ),
        in_specs=[vmem] * 6 + [smem],
        out_specs=(vmem, vmem, vmem),
        scratch_shapes=[
            pltpu.VMEM((lanes, n_out + 2 * half * cols), jnp.bfloat16),
            pltpu.VMEM((reach_y, views * planes, lanes), jnp.bfloat16),
            pltpu.VMEM((reach_y, reach_x * planes, views * planes), jnp.bfloat16),
            pltpu.VMEM((views * planes, n_out + 4 * half * cols), jnp.bfloat16),
        ],
    )(start, before, after, blur_b, corr_b, meas2, background)
    top = lax.ppermute(to_down, "gy", up)
    bottom = lax.ppermute(to_up, "gy", down)
    top = jnp.transpose(top.reshape(half, planes, cols), (1, 0, 2))
    bottom = jnp.transpose(bottom.reshape(half, planes, cols), (1, 0, 2))
    total = tot.at[:, :half].add(top).at[:, rows - half:].add(bottom)
    return start * total / views


def solution(mesh):
    in_specs = (P(None, None, ("parts", "gy"), None), P(None, ("parts", "gy"), None), P(), P())
    out_specs = P(None, ("parts", "gy"), None)
    return jax.shard_map(local, mesh=mesh, in_specs=in_specs, out_specs=out_specs, check_vma=False)
```

```python
import jax
import jax.numpy as jnp
from jax import lax
from jax.experimental import pallas as pl
from jax.experimental.pallas import tpu as pltpu
from jax.sharding import PartitionSpec as P


def build_bases(psf, planes, lanes, corr_lanes):
    kernel = psf / jnp.sum(psf, axis=(1, 2, 3), keepdims=True)
    views, depth, reach_y, reach_x = psf.shape
    half_z = depth // 2
    lane = jnp.arange(lanes, dtype=jnp.int32)
    tap = jnp.arange(depth, dtype=jnp.int32)
    col = jnp.arange(reach_x, dtype=jnp.int32)
    at = (col[None, :, None] * planes + half_z - tap[:, None, None]) % lanes
    onehot = (lane[None, None, :] == at).astype(jnp.float32)
    blur = jnp.einsum("vabc,acl->bvl", kernel, onehot, precision=lax.Precision.HIGHEST)
    view = jnp.arange(views, dtype=jnp.int32)
    at = (view[:, None, None] * planes + tap[None, :, None] - half_z) % corr_lanes
    onehot = (jnp.arange(corr_lanes, dtype=jnp.int32)[None, None, :] == at).astype(jnp.float32)
    corr = jnp.einsum("vabc,val->bcl", kernel, onehot, precision=lax.Precision.HIGHEST)
    return blur.astype(jnp.bfloat16), corr.astype(jnp.bfloat16)


def toeplitz_block(row, planes, half_z, width):
    lanes = row.shape[-1]
    blk = jnp.broadcast_to(row, (planes, lanes))
    blk = pltpu.roll(blk, 0, 1, stride=1, stride_axis=0)
    q = lax.broadcasted_iota(jnp.int32, (planes, lanes), 0)
    l = lax.broadcasted_iota(jnp.int32, (planes, lanes), 1)
    d = l % planes - q
    keep = (d <= half_z) & (d >= -half_z) & (l < width)
    return jnp.where(keep, blk, 0.0).astype(jnp.bfloat16)


def lane_shift(x, shift, cols):
    n = x.shape[-1]
    rolled = pltpu.roll(x, shift % n, x.ndim - 1) if shift % n else x
    col = lax.broadcasted_iota(jnp.int32, x.shape, x.ndim - 1) % cols
    keep = (col - shift >= 0) & (col - shift < cols)
    return jnp.where(keep, rolled, jnp.zeros_like(rolled))


def rl_kernel(start_ref, before_ref, after_ref, bbase_ref, cbase_ref, meas_ref, bg_ref, out_ref,
              xs_ref, wb_ref, wc_ref, rext_ref, *, cols, reach_y, reach_x, half, half_z):
    planes = start_ref.shape[0]
    n_out = start_ref.shape[1] * cols
    views = bbase_ref.shape[1]
    hw = half * cols
    n_mid = n_out + 2 * hw
    width = reach_x * planes
    for b in range(reach_y):
        for v in range(views):
            row = bbase_ref[b, v:v + 1, :].astype(jnp.float32)
            wb_ref[b, v * planes:(v + 1) * planes, :] = toeplitz_block(row, planes, half_z, width)
        for c in range(reach_x):
            row = cbase_ref[b, c:c + 1, :].astype(jnp.float32)
            wc_ref[b, c * planes:(c + 1) * planes, :] = toeplitz_block(row, planes, half_z, views * planes)
    rows = start_ref.shape[1]
    vp = views * planes
    m0 = 2 * half * planes

    def rounded_slab(e):
        if e < 2 * half:
            return before_ref[e * planes:(e + 1) * planes, :].astype(jnp.float32)
        if e >= 2 * half + rows:
            j = e - 2 * half - rows
            return after_ref[j * planes:(j + 1) * planes, :].astype(jnp.float32)
        return start_ref[:, e - 2 * half, :].astype(jnp.bfloat16).astype(jnp.float32)

    def measured_slab(m):
        if m < half:
            return before_ref[m0 + m * vp:m0 + (m + 1) * vp, :]
        if m >= half + rows:
            j = m - half - rows
            return after_ref[m0 + j * vp:m0 + (j + 1) * vp, :]
        return meas_ref[:, (m - half) * cols:(m - half + 1) * cols]

    xs_ref[width:, :] = jnp.zeros((xs_ref.shape[0] - width, xs_ref.shape[1]), jnp.bfloat16)
    for e in range(rows + 4 * half):
        slab = rounded_slab(e)
        for c in range(reach_x):
            xs_ref[c * planes:(c + 1) * planes, e * cols:(e + 1) * cols] = (
                lane_shift(slab, c - reach_x // 2, cols).astype(jnp.bfloat16))
    step = 2 * cols
    for k in range(n_mid // step):
        acc = None
        for b in range(reach_y):
            off = (2 * half - b) * cols + k * step
            part = jnp.dot(wb_ref[b], xs_ref[:, off:off + step], preferred_element_type=jnp.float32)
            acc = part if acc is None else acc + part
        for i in range(step // cols):
            m = k * (step // cols) + i
            meas = measured_slab(m)
            for v in range(views):
                rs = slice(v * planes, (v + 1) * planes)
                ratio = meas[rs].astype(jnp.float32) / (acc[rs, i * cols:(i + 1) * cols] + bg_ref[v])
                rext_ref[rs, m * cols:(m + 1) * cols] = ratio.astype(jnp.bfloat16)
    for k in range(n_out // step):
        acc = None
        for b in range(reach_y):
            off = b * cols + k * step
            part = jnp.dot(wc_ref[b], rext_ref[:, off:off + step], preferred_element_type=jnp.float32)
            acc = part if acc is None else acc + part
        total = None
        for c in range(reach_x):
            piece = lane_shift(acc[c * planes:(c + 1) * planes], reach_x // 2 - c, cols)
            total = piece if total is None else total + piece
        for i in range(step // cols):
            r = k * (step // cols) + i
            out_ref[:, r, :] = start_ref[:, r, :] * total[:, i * cols:(i + 1) * cols] / views


def local(measured, start, psf, background):
    planes, rows, cols = start.shape
    views = measured.shape[0]
    reach_y, reach_x = psf.shape[2], psf.shape[3]
    half = reach_y // 2
    half_z = psf.shape[1] // 2
    assert rows >= 2 * half and rows % 2 == 0
    lanes = -(-(reach_x * planes + half_z) // 128) * 128
    blur_b, corr_b = build_bases(psf, planes, lanes, views * planes)
    n_out = rows * cols
    hw = half * cols
    vmem = pl.BlockSpec(memory_space=pltpu.VMEM)
    smem = pl.BlockSpec(memory_space=pltpu.SMEM)

    rounded = start.astype(jnp.bfloat16)
    meas2 = measured.reshape(views * planes, n_out)

    def slab(lo, hi):
        r = jnp.transpose(rounded[:, lo:hi, :], (1, 0, 2)).reshape(-1, cols)
        return r

    def meas_rows(lo, hi):
        m = jnp.transpose(measured[:, :, lo:hi, :], (2, 0, 1, 3)).reshape(-1, cols)
        return m

    last = jnp.concatenate([slab(rows - 2 * half, rows), meas_rows(rows - half, rows)], axis=0)
    first = jnp.concatenate([slab(0, 2 * half), meas_rows(0, half)], axis=0)
    peers = lax.axis_size("gy")
    before = lax.ppermute(last, "gy", [(i, i + 1) for i in range(peers - 1)])
    after = lax.ppermute(first, "gy", [(i + 1, i) for i in range(peers - 1)])

    n_mid = n_out + 2 * hw
    est = pl.pallas_call(
        lambda *refs: rl_kernel(*refs, cols=cols, reach_y=reach_y, reach_x=reach_x, half=half, half_z=half_z),
        out_shape=jax.ShapeDtypeStruct((planes, rows, cols), jnp.float32),
        in_specs=[vmem] * 6 + [smem],
        out_specs=vmem,
        scratch_shapes=[
            pltpu.VMEM((lanes, n_out + 4 * hw), jnp.bfloat16),
            pltpu.VMEM((reach_y, views * planes, lanes), jnp.bfloat16),
            pltpu.VMEM((reach_y, reach_x * planes, views * planes), jnp.bfloat16),
            pltpu.VMEM((views * planes, n_mid), jnp.bfloat16),
        ],
    )(*[pltpu.with_memory_space_constraint(x, pltpu.VMEM) for x in (start, before, after, blur_b, corr_b, meas2)],
      background)
    return est


def solution(mesh):
    in_specs = (P(None, None, ("parts", "gy"), None), P(None, ("parts", "gy"), None), P(), P())
    out_specs = P(None, ("parts", "gy"), None)
    return jax.shard_map(local, mesh=mesh, in_specs=in_specs, out_specs=out_specs, check_vma=False)
```

```python
import jax
import jax.numpy as jnp
from jax import lax
from jax.experimental import pallas as pl
from jax.experimental.pallas import tpu as pltpu
from jax.sharding import PartitionSpec as P


def build_bases(psf, planes, lanes, corr_lanes):
    kernel = psf / jnp.sum(psf, axis=(1, 2, 3), keepdims=True)
    views, depth, reach_y, reach_x = psf.shape
    half_z = depth // 2
    lane = jnp.arange(lanes, dtype=jnp.int32)
    tap = jnp.arange(depth, dtype=jnp.int32)
    col = jnp.arange(reach_x, dtype=jnp.int32)
    at = (col[None, :, None] * planes + half_z - tap[:, None, None]) % lanes
    onehot = (lane[None, None, :] == at).astype(jnp.float32)
    blur = jnp.einsum("vabc,acl->bvl", kernel, onehot, precision=lax.Precision.HIGHEST)
    view = jnp.arange(views, dtype=jnp.int32)
    at = (view[:, None, None] * planes + tap[None, :, None] - half_z) % corr_lanes
    onehot = (jnp.arange(corr_lanes, dtype=jnp.int32)[None, None, :] == at).astype(jnp.float32)
    corr = jnp.einsum("vabc,val->bcl", kernel, onehot, precision=lax.Precision.HIGHEST)
    return blur.astype(jnp.bfloat16), corr.astype(jnp.bfloat16)


def toeplitz_block(row, planes, half_z, width):
    lanes = row.shape[-1]
    blk = jnp.broadcast_to(row, (planes, lanes))
    blk = pltpu.roll(blk, 0, 1, stride=1, stride_axis=0)
    q = lax.broadcasted_iota(jnp.int32, (planes, lanes), 0)
    l = lax.broadcasted_iota(jnp.int32, (planes, lanes), 1)
    d = l % planes - q
    keep = (d <= half_z) & (d >= -half_z) & (l < width)
    return jnp.where(keep, blk, 0.0).astype(jnp.bfloat16)


def lane_shift(x, shift, cols):
    n = x.shape[-1]
    rolled = pltpu.roll(x, shift % n, x.ndim - 1) if shift % n else x
    col = lax.broadcasted_iota(jnp.int32, x.shape, x.ndim - 1) % cols
    keep = (col - shift >= 0) & (col - shift < cols)
    return jnp.where(keep, rolled, jnp.zeros_like(rolled))


def rl_kernel(start_ref, before_ref, after_ref, bbase_ref, cbase_ref, meas_ref, bg_ref, out_ref,
              xs_ref, wb_ref, wc_ref, rext_ref, *, cols, reach_y, reach_x, half, half_z):
    planes = start_ref.shape[0]
    n_out = start_ref.shape[1] * cols
    views = bbase_ref.shape[1]
    hw = half * cols
    n_mid = n_out + 2 * hw
    width = reach_x * planes
    for b in range(reach_y):
        for v in range(views):
            row = bbase_ref[b, v:v + 1, :].astype(jnp.float32)
            wb_ref[b, v * planes:(v + 1) * planes, :] = toeplitz_block(row, planes, half_z, width)
        for c in range(reach_x):
            row = cbase_ref[b, c:c + 1, :].astype(jnp.float32)
            wc_ref[b, c * planes:(c + 1) * planes, :] = toeplitz_block(row, planes, half_z, views * planes)
    rows = start_ref.shape[1]
    vp = views * planes
    m0 = 2 * half * planes

    def rounded_slab(e):
        if e < 2 * half:
            return before_ref[e * planes:(e + 1) * planes, :].astype(jnp.float32)
        if e >= 2 * half + rows:
            j = e - 2 * half - rows
            return after_ref[j * planes:(j + 1) * planes, :].astype(jnp.float32)
        return start_ref[:, e - 2 * half, :].astype(jnp.bfloat16).astype(jnp.float32)

    def measured_slab(m):
        if m < half:
            return before_ref[m0 + m * vp:m0 + (m + 1) * vp, :]
        if m >= half + rows:
            j = m - half - rows
            return after_ref[m0 + j * vp:m0 + (j + 1) * vp, :]
        return meas_ref[:, (m - half) * cols:(m - half + 1) * cols]

    xs_ref[width:, :] = jnp.zeros((xs_ref.shape[0] - width, xs_ref.shape[1]), jnp.bfloat16)
    for e in range(rows + 4 * half):
        slab = rounded_slab(e)
        for c in range(reach_x):
            xs_ref[c * planes:(c + 1) * planes, e * cols:(e + 1) * cols] = (
                lane_shift(slab, c - reach_x // 2, cols).astype(jnp.bfloat16))
    step = 2 * cols
    for k in range(n_mid // step):
        acc = None
        for b in range(reach_y):
            off = (2 * half - b) * cols + k * step
            part = jnp.dot(wb_ref[b], xs_ref[:, off:off + step], preferred_element_type=jnp.float32)
            acc = part if acc is None else acc + part
        for i in range(step // cols):
            m = k * (step // cols) + i
            meas = measured_slab(m)
            for v in range(views):
                rs = slice(v * planes, (v + 1) * planes)
                ratio = meas[rs].astype(jnp.float32) / (acc[rs, i * cols:(i + 1) * cols] + bg_ref[v])
                rext_ref[rs, m * cols:(m + 1) * cols] = ratio.astype(jnp.bfloat16)
    for k in range(n_out // step):
        acc = None
        for b in range(reach_y):
            off = b * cols + k * step
            part = jnp.dot(wc_ref[b], rext_ref[:, off:off + step], preferred_element_type=jnp.float32)
            acc = part if acc is None else acc + part
        total = None
        for c in range(reach_x):
            piece = lane_shift(acc[c * planes:(c + 1) * planes], reach_x // 2 - c, cols)
            total = piece if total is None else total + piece
        for i in range(step // cols):
            r = k * (step // cols) + i
            out_ref[:, r, :] = start_ref[:, r, :] * total[:, i * cols:(i + 1) * cols] / views


def local(measured, start, psf, background):
    planes, rows, cols = start.shape
    views = measured.shape[0]
    reach_y, reach_x = psf.shape[2], psf.shape[3]
    half = reach_y // 2
    half_z = psf.shape[1] // 2
    assert rows >= 2 * half and rows % 2 == 0
    lanes = -(-(reach_x * planes + half_z) // 128) * 128
    blur_b, corr_b = build_bases(psf, planes, lanes, views * planes)
    n_out = rows * cols
    hw = half * cols
    vmem = pl.BlockSpec(memory_space=pltpu.VMEM)
    smem = pl.BlockSpec(memory_space=pltpu.SMEM)

    meas2 = measured.reshape(views * planes, n_out)

    def slab(lo, hi):
        r = jnp.concatenate([start[:, i, :].astype(jnp.bfloat16) for i in range(lo, hi)], axis=0)
        return r

    def meas_rows(lo, hi):
        m = jnp.concatenate([measured[:, :, r, :].reshape(-1, cols) for r in range(lo, hi)], axis=0)
        return m

    last = jnp.concatenate([slab(rows - 2 * half, rows), meas_rows(rows - half, rows)], axis=0)
    first = jnp.concatenate([slab(0, 2 * half), meas_rows(0, half)], axis=0)
    peers = lax.axis_size("gy")
    before = lax.ppermute(last, "gy", [(i, i + 1) for i in range(peers - 1)])
    after = lax.ppermute(first, "gy", [(i + 1, i) for i in range(peers - 1)])

    n_mid = n_out + 2 * hw
    est = pl.pallas_call(
        lambda *refs: rl_kernel(*refs, cols=cols, reach_y=reach_y, reach_x=reach_x, half=half, half_z=half_z),
        out_shape=jax.ShapeDtypeStruct((planes, rows, cols), jnp.float32),
        in_specs=[vmem] * 6 + [smem],
        out_specs=vmem,
        scratch_shapes=[
            pltpu.VMEM((lanes, n_out + 4 * hw), jnp.bfloat16),
            pltpu.VMEM((reach_y, views * planes, lanes), jnp.bfloat16),
            pltpu.VMEM((reach_y, reach_x * planes, views * planes), jnp.bfloat16),
            pltpu.VMEM((views * planes, n_mid), jnp.bfloat16),
        ],
    )(*[pltpu.with_memory_space_constraint(x, pltpu.VMEM) for x in (start, before, after, blur_b, corr_b, meas2)],
      background)
    return est


def solution(mesh):
    in_specs = (P(None, None, ("parts", "gy"), None), P(None, ("parts", "gy"), None), P(), P())
    out_specs = P(None, ("parts", "gy"), None)
    return jax.shard_map(local, mesh=mesh, in_specs=in_specs, out_specs=out_specs, check_vma=False)
```

```python
import jax
import jax.numpy as jnp
from jax import lax
from jax.experimental import pallas as pl
from jax.experimental.pallas import tpu as pltpu
from jax.sharding import PartitionSpec as P


def build_bases(psf, planes, lanes, corr_lanes):
    kernel = psf / jnp.sum(psf, axis=(1, 2, 3), keepdims=True)
    views, depth, reach_y, reach_x = psf.shape
    half_z = depth // 2
    lane = jnp.arange(lanes, dtype=jnp.int32)
    tap = jnp.arange(depth, dtype=jnp.int32)
    col = jnp.arange(reach_x, dtype=jnp.int32)
    at = (col[None, :, None] * planes + half_z - tap[:, None, None]) % lanes
    onehot = (lane[None, None, :] == at).astype(jnp.float32)
    blur = jnp.einsum("vabc,acl->bvl", kernel, onehot, precision=lax.Precision.HIGHEST)
    view = jnp.arange(views, dtype=jnp.int32)
    at = (view[:, None, None] * planes + tap[None, :, None] - half_z) % corr_lanes
    onehot = (jnp.arange(corr_lanes, dtype=jnp.int32)[None, None, :] == at).astype(jnp.float32)
    corr = jnp.einsum("vabc,val->bcl", kernel, onehot, precision=lax.Precision.HIGHEST)
    return blur.astype(jnp.bfloat16), corr.astype(jnp.bfloat16)


def toeplitz_block(row, planes, half_z, width):
    lanes = row.shape[-1]
    blk = jnp.broadcast_to(row, (planes, lanes))
    blk = pltpu.roll(blk, 0, 1, stride=1, stride_axis=0)
    q = lax.broadcasted_iota(jnp.int32, (planes, lanes), 0)
    l = lax.broadcasted_iota(jnp.int32, (planes, lanes), 1)
    d = l % planes - q
    keep = (d <= half_z) & (d >= -half_z) & (l < width)
    return jnp.where(keep, blk, 0.0).astype(jnp.bfloat16)


def lane_shift(x, shift, cols):
    n = x.shape[-1]
    rolled = pltpu.roll(x, shift % n, x.ndim - 1) if shift % n else x
    col = lax.broadcasted_iota(jnp.int32, x.shape, x.ndim - 1) % cols
    keep = (col - shift >= 0) & (col - shift < cols)
    return jnp.where(keep, rolled, jnp.zeros_like(rolled))


def weights_kernel(bbase_ref, cbase_ref, wb_ref, wc_ref, *, planes, half_z, width):
    reach_y, views = bbase_ref.shape[0], bbase_ref.shape[1]
    reach_x = cbase_ref.shape[1]
    for b in range(reach_y):
        for v in range(views):
            row = bbase_ref[b, v:v + 1, :].astype(jnp.float32)
            wb_ref[b, v * planes:(v + 1) * planes, :] = toeplitz_block(row, planes, half_z, width)
        for c in range(reach_x):
            row = cbase_ref[b, c:c + 1, :].astype(jnp.float32)
            wc_ref[b, c * planes:(c + 1) * planes, :] = toeplitz_block(row, planes, half_z, views * planes)


def rl_kernel(start_ref, before_ref, after_ref, wb_ref, wc_ref, meas_ref, bg_ref, out_ref,
              xs_ref, rext_ref, *, cols, reach_y, reach_x, half, half_z):
    planes = start_ref.shape[0]
    n_out = start_ref.shape[1] * cols
    views = meas_ref.shape[0] // planes
    hw = half * cols
    n_mid = n_out + 2 * hw
    width = reach_x * planes
    rows = start_ref.shape[1]
    vp = views * planes
    m0 = 2 * half * planes

    def rounded_slab(e):
        if e < 2 * half:
            return before_ref[e * planes:(e + 1) * planes, :].astype(jnp.float32)
        if e >= 2 * half + rows:
            j = e - 2 * half - rows
            return after_ref[j * planes:(j + 1) * planes, :].astype(jnp.float32)
        return start_ref[:, e - 2 * half, :].astype(jnp.bfloat16).astype(jnp.float32)

    def measured_slab(m):
        if m < half:
            return before_ref[m0 + m * vp:m0 + (m + 1) * vp, :]
        if m >= half + rows:
            j = m - half - rows
            return after_ref[m0 + j * vp:m0 + (j + 1) * vp, :]
        return meas_ref[:, (m - half) * cols:(m - half + 1) * cols]

    xs_ref[width:, :] = jnp.zeros((xs_ref.shape[0] - width, xs_ref.shape[1]), jnp.bfloat16)
    for e in range(rows + 4 * half):
        slab = rounded_slab(e)
        for c in range(reach_x):
            xs_ref[c * planes:(c + 1) * planes, e * cols:(e + 1) * cols] = (
                lane_shift(slab, c - reach_x // 2, cols).astype(jnp.bfloat16))
    step = 2 * cols
    for k in range(n_mid // step):
        acc = None
        for b in range(reach_y):
            off = (2 * half - b) * cols + k * step
            part = jnp.dot(wb_ref[b], xs_ref[:, off:off + step], preferred_element_type=jnp.float32)
            acc = part if acc is None else acc + part
        for i in range(step // cols):
            m = k * (step // cols) + i
            meas = measured_slab(m)
            for v in range(views):
                rs = slice(v * planes, (v + 1) * planes)
                ratio = meas[rs].astype(jnp.float32) / (acc[rs, i * cols:(i + 1) * cols] + bg_ref[v])
                rext_ref[rs, m * cols:(m + 1) * cols] = ratio.astype(jnp.bfloat16)
    for k in range(n_out // step):
        acc = None
        for b in range(reach_y):
            off = b * cols + k * step
            part = jnp.dot(wc_ref[b], rext_ref[:, off:off + step], preferred_element_type=jnp.float32)
            acc = part if acc is None else acc + part
        total = None
        for c in range(reach_x):
            piece = lane_shift(acc[c * planes:(c + 1) * planes], reach_x // 2 - c, cols)
            total = piece if total is None else total + piece
        for i in range(step // cols):
            r = k * (step // cols) + i
            out_ref[:, r, :] = start_ref[:, r, :] * total[:, i * cols:(i + 1) * cols] / views


def local(measured, start, psf, background):
    planes, rows, cols = start.shape
    views = measured.shape[0]
    reach_y, reach_x = psf.shape[2], psf.shape[3]
    half = reach_y // 2
    half_z = psf.shape[1] // 2
    assert rows >= 2 * half and rows % 2 == 0
    lanes = -(-(reach_x * planes + half_z) // 128) * 128
    blur_b, corr_b = build_bases(psf, planes, lanes, views * planes)
    n_out = rows * cols
    hw = half * cols
    vmem = pl.BlockSpec(memory_space=pltpu.VMEM)
    smem = pl.BlockSpec(memory_space=pltpu.SMEM)

    rounded = start.astype(jnp.bfloat16)
    meas2 = measured.reshape(views * planes, n_out)

    def slab(lo, hi):
        r = jnp.transpose(rounded[:, lo:hi, :], (1, 0, 2)).reshape(-1, cols)
        return r

    def meas_rows(lo, hi):
        m = jnp.transpose(measured[:, :, lo:hi, :], (2, 0, 1, 3)).reshape(-1, cols)
        return m

    last = jnp.concatenate([slab(rows - 2 * half, rows), meas_rows(rows - half, rows)], axis=0)
    first = jnp.concatenate([slab(0, 2 * half), meas_rows(0, half)], axis=0)
    peers = lax.axis_size("gy")
    before = lax.ppermute(last, "gy", [(i, i + 1) for i in range(peers - 1)])
    after = lax.ppermute(first, "gy", [(i + 1, i) for i in range(peers - 1)])

    n_mid = n_out + 2 * hw
    wb, wc = pl.pallas_call(
        lambda *refs: weights_kernel(*refs, planes=planes, half_z=half_z, width=reach_x * planes),
        out_shape=(
            jax.ShapeDtypeStruct((reach_y, views * planes, lanes), jnp.bfloat16),
            jax.ShapeDtypeStruct((reach_y, reach_x * planes, views * planes), jnp.bfloat16),
        ),
        in_specs=[vmem] * 2,
        out_specs=(vmem, vmem),
    )(*[pltpu.with_memory_space_constraint(x, pltpu.VMEM) for x in (blur_b, corr_b)])
    est = pl.pallas_call(
        lambda *refs: rl_kernel(*refs, cols=cols, reach_y=reach_y, reach_x=reach_x, half=half, half_z=half_z),
        out_shape=jax.ShapeDtypeStruct((planes, rows, cols), jnp.float32),
        in_specs=[vmem] * 6 + [smem],
        out_specs=vmem,
        scratch_shapes=[
            pltpu.VMEM((lanes, n_out + 4 * hw), jnp.bfloat16),
            pltpu.VMEM((views * planes, n_mid), jnp.bfloat16),
        ],
    )(*[pltpu.with_memory_space_constraint(x, pltpu.VMEM) for x in (start, before, after, wb, wc, meas2)],
      background)
    return est


def solution(mesh):
    in_specs = (P(None, None, ("parts", "gy"), None), P(None, ("parts", "gy"), None), P(), P())
    out_specs = P(None, ("parts", "gy"), None)
    return jax.shard_map(local, mesh=mesh, in_specs=in_specs, out_specs=out_specs, check_vma=False)
```

```python
import jax
import jax.numpy as jnp
from jax import lax
from jax.experimental import pallas as pl
from jax.experimental.pallas import tpu as pltpu
from jax.sharding import PartitionSpec as P


def build_bases(psf, planes, lanes, corr_lanes):
    kernel = psf / jnp.sum(psf, axis=(1, 2, 3), keepdims=True)
    views, depth, reach_y, reach_x = psf.shape
    half_z = depth // 2
    lane = jnp.arange(lanes, dtype=jnp.int32)
    tap = jnp.arange(depth, dtype=jnp.int32)
    col = jnp.arange(reach_x, dtype=jnp.int32)
    at = (col[None, :, None] * planes + half_z - tap[:, None, None]) % lanes
    onehot = (lane[None, None, :] == at).astype(jnp.float32)
    blur = jnp.einsum("vabc,acl->bvl", kernel, onehot, precision=lax.Precision.HIGHEST)
    view = jnp.arange(views, dtype=jnp.int32)
    at = (view[:, None, None] * planes + tap[None, :, None] - half_z) % corr_lanes
    onehot = (jnp.arange(corr_lanes, dtype=jnp.int32)[None, None, :] == at).astype(jnp.float32)
    corr = jnp.einsum("vabc,val->bcl", kernel, onehot, precision=lax.Precision.HIGHEST)
    return blur.astype(jnp.bfloat16), corr.astype(jnp.bfloat16)


def toeplitz_block(row, planes, half_z, width):
    lanes = row.shape[-1]
    blk = jnp.broadcast_to(row, (planes, lanes))
    blk = pltpu.roll(blk, 0, 1, stride=1, stride_axis=0)
    q = lax.broadcasted_iota(jnp.int32, (planes, lanes), 0)
    l = lax.broadcasted_iota(jnp.int32, (planes, lanes), 1)
    d = l % planes - q
    keep = (d <= half_z) & (d >= -half_z) & (l < width)
    return jnp.where(keep, blk, 0.0).astype(jnp.bfloat16)


def lane_shift(x, shift, cols):
    n = x.shape[-1]
    rolled = pltpu.roll(x, shift % n, x.ndim - 1) if shift % n else x
    col = lax.broadcasted_iota(jnp.int32, x.shape, x.ndim - 1) % cols
    keep = (col - shift >= 0) & (col - shift < cols)
    return jnp.where(keep, rolled, jnp.zeros_like(rolled))


def weights_kernel(bbase_ref, cbase_ref, wb_ref, wc_ref, *, planes, half_z, width):
    reach_y, views = bbase_ref.shape[0], bbase_ref.shape[1]
    reach_x = cbase_ref.shape[1]
    for b in range(reach_y):
        for v in range(views):
            row = bbase_ref[b, v:v + 1, :].astype(jnp.float32)
            wb_ref[b, v * planes:(v + 1) * planes, :] = toeplitz_block(row, planes, half_z, width)
        for c in range(reach_x):
            row = cbase_ref[b, c:c + 1, :].astype(jnp.float32)
            wc_ref[b, c * planes:(c + 1) * planes, :] = toeplitz_block(row, planes, half_z, views * planes)


def rl_kernel(start_ref, before_ref, after_ref, wb_hbm, wc_hbm, meas_ref, bg_ref, out_ref,
              xs_ref, rext_ref, wb_ref, wc_ref, sems, *, cols, reach_y, reach_x, half, half_z):
    copy_b = pltpu.make_async_copy(wb_hbm, wb_ref, sems.at[0])
    copy_c = pltpu.make_async_copy(wc_hbm, wc_ref, sems.at[1])
    copy_b.start()
    copy_c.start()
    planes = start_ref.shape[0]
    n_out = start_ref.shape[1] * cols
    views = meas_ref.shape[0] // planes
    hw = half * cols
    n_mid = n_out + 2 * hw
    width = reach_x * planes
    rows = start_ref.shape[1]
    vp = views * planes
    m0 = 2 * half * planes

    def rounded_slab(e):
        if e < 2 * half:
            return before_ref[e * planes:(e + 1) * planes, :].astype(jnp.float32)
        if e >= 2 * half + rows:
            j = e - 2 * half - rows
            return after_ref[j * planes:(j + 1) * planes, :].astype(jnp.float32)
        return start_ref[:, e - 2 * half, :].astype(jnp.bfloat16).astype(jnp.float32)

    def measured_slab(m):
        if m < half:
            return before_ref[m0 + m * vp:m0 + (m + 1) * vp, :]
        if m >= half + rows:
            j = m - half - rows
            return after_ref[m0 + j * vp:m0 + (j + 1) * vp, :]
        return meas_ref[:, (m - half) * cols:(m - half + 1) * cols]

    xs_ref[width:, :] = jnp.zeros((xs_ref.shape[0] - width, xs_ref.shape[1]), jnp.bfloat16)
    for e in range(rows + 4 * half):
        slab = rounded_slab(e)
        for c in range(reach_x):
            xs_ref[c * planes:(c + 1) * planes, e * cols:(e + 1) * cols] = (
                lane_shift(slab, c - reach_x // 2, cols).astype(jnp.bfloat16))
    copy_b.wait()
    step = 2 * cols
    for k in range(n_mid // step):
        acc = None
        for b in range(reach_y):
            off = (2 * half - b) * cols + k * step
            part = jnp.dot(wb_ref[b], xs_ref[:, off:off + step], preferred_element_type=jnp.float32)
            acc = part if acc is None else acc + part
        for i in range(step // cols):
            m = k * (step // cols) + i
            meas = measured_slab(m)
            for v in range(views):
                rs = slice(v * planes, (v + 1) * planes)
                ratio = meas[rs].astype(jnp.float32) / (acc[rs, i * cols:(i + 1) * cols] + bg_ref[v])
                rext_ref[rs, m * cols:(m + 1) * cols] = ratio.astype(jnp.bfloat16)
    copy_c.wait()
    for k in range(n_out // step):
        acc = None
        for b in range(reach_y):
            off = b * cols + k * step
            part = jnp.dot(wc_ref[b], rext_ref[:, off:off + step], preferred_element_type=jnp.float32)
            acc = part if acc is None else acc + part
        total = None
        for c in range(reach_x):
            piece = lane_shift(acc[c * planes:(c + 1) * planes], reach_x // 2 - c, cols)
            total = piece if total is None else total + piece
        for i in range(step // cols):
            r = k * (step // cols) + i
            out_ref[:, r, :] = start_ref[:, r, :] * total[:, i * cols:(i + 1) * cols] / views


def local(measured, start, psf, background):
    planes, rows, cols = start.shape
    views = measured.shape[0]
    reach_y, reach_x = psf.shape[2], psf.shape[3]
    half = reach_y // 2
    half_z = psf.shape[1] // 2
    assert rows >= 2 * half and rows % 2 == 0
    lanes = -(-(reach_x * planes + half_z) // 128) * 128
    blur_b, corr_b = build_bases(psf, planes, lanes, views * planes)
    n_out = rows * cols
    hw = half * cols
    vmem = pl.BlockSpec(memory_space=pltpu.VMEM)
    smem = pl.BlockSpec(memory_space=pltpu.SMEM)

    rounded = start.astype(jnp.bfloat16)
    meas2 = measured.reshape(views * planes, n_out)

    def slab(lo, hi):
        r = jnp.transpose(rounded[:, lo:hi, :], (1, 0, 2)).reshape(-1, cols)
        return r

    def meas_rows(lo, hi):
        m = jnp.transpose(measured[:, :, lo:hi, :], (2, 0, 1, 3)).reshape(-1, cols)
        return m

    last = jnp.concatenate([slab(rows - 2 * half, rows), meas_rows(rows - half, rows)], axis=0)
    first = jnp.concatenate([slab(0, 2 * half), meas_rows(0, half)], axis=0)
    peers = lax.axis_size("gy")
    before = lax.ppermute(last, "gy", [(i, i + 1) for i in range(peers - 1)])
    after = lax.ppermute(first, "gy", [(i + 1, i) for i in range(peers - 1)])

    n_mid = n_out + 2 * hw
    wb, wc = pl.pallas_call(
        lambda *refs: weights_kernel(*refs, planes=planes, half_z=half_z, width=reach_x * planes),
        out_shape=(
            jax.ShapeDtypeStruct((reach_y, views * planes, lanes), jnp.bfloat16),
            jax.ShapeDtypeStruct((reach_y, reach_x * planes, views * planes), jnp.bfloat16),
        ),
        in_specs=[vmem] * 2,
        out_specs=(vmem, vmem),
    )(*[pltpu.with_memory_space_constraint(x, pltpu.VMEM) for x in (blur_b, corr_b)])
    est = pl.pallas_call(
        lambda *refs: rl_kernel(*refs, cols=cols, reach_y=reach_y, reach_x=reach_x, half=half, half_z=half_z),
        out_shape=jax.ShapeDtypeStruct((planes, rows, cols), jnp.float32),
        in_specs=[vmem] * 3 + [pl.BlockSpec(memory_space=pl.ANY)] * 2 + [vmem, smem],
        out_specs=vmem,
        scratch_shapes=[
            pltpu.VMEM((lanes, n_out + 4 * hw), jnp.bfloat16),
            pltpu.VMEM((views * planes, n_mid), jnp.bfloat16),
            pltpu.VMEM(wb.shape, jnp.bfloat16),
            pltpu.VMEM(wc.shape, jnp.bfloat16),
            pltpu.SemaphoreType.DMA((2,)),
        ],
    )(*[pltpu.with_memory_space_constraint(x, pltpu.VMEM) for x in (start, before, after)], wb, wc,
      pltpu.with_memory_space_constraint(meas2, pltpu.VMEM),
      background)
    return est


def solution(mesh):
    in_specs = (P(None, None, ("parts", "gy"), None), P(None, ("parts", "gy"), None), P(), P())
    out_specs = P(None, ("parts", "gy"), None)
    return jax.shard_map(local, mesh=mesh, in_specs=in_specs, out_specs=out_specs, check_vma=False)
```

```python
import jax
import jax.numpy as jnp
from jax import lax
from jax.experimental import pallas as pl
from jax.experimental.pallas import tpu as pltpu
from jax.sharding import PartitionSpec as P


def build_bases(psf, planes, lanes, corr_lanes):
    kernel = psf / jnp.sum(psf, axis=(1, 2, 3), keepdims=True)
    views, depth, reach_y, reach_x = psf.shape
    half_z = depth // 2
    lane = jnp.arange(lanes, dtype=jnp.int32)
    tap = jnp.arange(depth, dtype=jnp.int32)
    col = jnp.arange(reach_x, dtype=jnp.int32)
    at = (col[None, :, None] * planes + half_z - tap[:, None, None]) % lanes
    onehot = (lane[None, None, :] == at).astype(jnp.float32)
    blur = jnp.einsum("vabc,acl->bvl", kernel, onehot, precision=lax.Precision.HIGHEST)
    view = jnp.arange(views, dtype=jnp.int32)
    at = (view[:, None, None] * planes + tap[None, :, None] - half_z) % corr_lanes
    onehot = (jnp.arange(corr_lanes, dtype=jnp.int32)[None, None, :] == at).astype(jnp.float32)
    corr = jnp.einsum("vabc,val->bcl", kernel, onehot, precision=lax.Precision.HIGHEST)
    return blur.astype(jnp.bfloat16), corr.astype(jnp.bfloat16)


def toeplitz_block(row, planes, half_z, width):
    lanes = row.shape[-1]
    blk = jnp.broadcast_to(row, (planes, lanes))
    blk = pltpu.roll(blk, 0, 1, stride=1, stride_axis=0)
    q = lax.broadcasted_iota(jnp.int32, (planes, lanes), 0)
    l = lax.broadcasted_iota(jnp.int32, (planes, lanes), 1)
    d = l % planes - q
    keep = (d <= half_z) & (d >= -half_z) & (l < width)
    return jnp.where(keep, blk, jnp.zeros_like(blk))


def lane_shift(x, shift, cols):
    n = x.shape[-1]
    rolled = pltpu.roll(x, shift % n, x.ndim - 1) if shift % n else x
    col = lax.broadcasted_iota(jnp.int32, x.shape, x.ndim - 1) % cols
    keep = (col - shift >= 0) & (col - shift < cols)
    return jnp.where(keep, rolled, jnp.zeros_like(rolled))


def rl_kernel(start_ref, before_ref, after_ref, bbase_ref, cbase_ref, meas_ref, bg_ref, out_ref,
              xs_ref, wb_ref, wc_ref, rext_ref, *, cols, reach_y, reach_x, half, half_z):
    planes = start_ref.shape[0]
    n_out = start_ref.shape[1] * cols
    views = bbase_ref.shape[1]
    hw = half * cols
    n_mid = n_out + 2 * hw
    width = reach_x * planes
    for b in range(reach_y):
        for v in range(views):
            row = bbase_ref[b, v:v + 1, :]
            wb_ref[b, v * planes:(v + 1) * planes, :] = toeplitz_block(row, planes, half_z, width)
        for c in range(reach_x):
            row = cbase_ref[b, c:c + 1, :]
            wc_ref[b, c * planes:(c + 1) * planes, :] = toeplitz_block(row, planes, half_z, views * planes)
    rows = start_ref.shape[1]
    vp = views * planes
    m0 = 2 * half * planes

    def rounded_slab(e):
        if e < 2 * half:
            return before_ref[e * planes:(e + 1) * planes, :]
        if e >= 2 * half + rows:
            j = e - 2 * half - rows
            return after_ref[j * planes:(j + 1) * planes, :]
        return start_ref[:, e - 2 * half, :].astype(jnp.bfloat16)

    def measured_slab(m):
        if m < half:
            return before_ref[m0 + m * vp:m0 + (m + 1) * vp, :]
        if m >= half + rows:
            j = m - half - rows
            return after_ref[m0 + j * vp:m0 + (j + 1) * vp, :]
        return meas_ref[:, (m - half) * cols:(m - half + 1) * cols]

    xs_ref[width:, :] = jnp.zeros((xs_ref.shape[0] - width, xs_ref.shape[1]), jnp.bfloat16)
    for e in range(rows + 4 * half):
        slab = rounded_slab(e)
        for c in range(reach_x):
            xs_ref[c * planes:(c + 1) * planes, e * cols:(e + 1) * cols] = lane_shift(slab, c - reach_x // 2, cols)
    step = 2 * cols
    for k in range(n_mid // step):
        acc = None
        for b in range(reach_y):
            off = (2 * half - b) * cols + k * step
            part = jnp.dot(wb_ref[b], xs_ref[:, off:off + step], preferred_element_type=jnp.float32)
            acc = part if acc is None else acc + part
        for i in range(step // cols):
            m = k * (step // cols) + i
            meas = measured_slab(m)
            for v in range(views):
                rs = slice(v * planes, (v + 1) * planes)
                ratio = meas[rs].astype(jnp.float32) / (acc[rs, i * cols:(i + 1) * cols] + bg_ref[v])
                rext_ref[rs, m * cols:(m + 1) * cols] = ratio.astype(jnp.bfloat16)
    for k in range(n_out // step):
        acc = None
        for b in range(reach_y):
            off = b * cols + k * step
            part = jnp.dot(wc_ref[b], rext_ref[:, off:off + step], preferred_element_type=jnp.float32)
            acc = part if acc is None else acc + part
        total = None
        for c in range(reach_x):
            piece = lane_shift(acc[c * planes:(c + 1) * planes], reach_x // 2 - c, cols)
            total = piece if total is None else total + piece
        for i in range(step // cols):
            r = k * (step // cols) + i
            out_ref[:, r, :] = start_ref[:, r, :] * total[:, i * cols:(i + 1) * cols] / views


def local(measured, start, psf, background):
    planes, rows, cols = start.shape
    views = measured.shape[0]
    reach_y, reach_x = psf.shape[2], psf.shape[3]
    half = reach_y // 2
    half_z = psf.shape[1] // 2
    assert rows >= 2 * half and rows % 2 == 0
    lanes = -(-(reach_x * planes + half_z) // 128) * 128
    blur_b, corr_b = build_bases(psf, planes, lanes, views * planes)
    n_out = rows * cols
    hw = half * cols
    vmem = pl.BlockSpec(memory_space=pltpu.VMEM)
    smem = pl.BlockSpec(memory_space=pltpu.SMEM)

    rounded = start.astype(jnp.bfloat16)
    meas2 = measured.reshape(views * planes, n_out)

    def slab(lo, hi):
        r = jnp.transpose(rounded[:, lo:hi, :], (1, 0, 2)).reshape(-1, cols)
        return r

    def meas_rows(lo, hi):
        m = jnp.transpose(measured[:, :, lo:hi, :], (2, 0, 1, 3)).reshape(-1, cols)
        return m

    last = jnp.concatenate([slab(rows - 2 * half, rows), meas_rows(rows - half, rows)], axis=0)
    first = jnp.concatenate([slab(0, 2 * half), meas_rows(0, half)], axis=0)
    peers = lax.axis_size("gy")
    before = lax.ppermute(last, "gy", [(i, i + 1) for i in range(peers - 1)])
    after = lax.ppermute(first, "gy", [(i + 1, i) for i in range(peers - 1)])

    n_mid = n_out + 2 * hw
    est = pl.pallas_call(
        lambda *refs: rl_kernel(*refs, cols=cols, reach_y=reach_y, reach_x=reach_x, half=half, half_z=half_z),
        out_shape=jax.ShapeDtypeStruct((planes, rows, cols), jnp.float32),
        in_specs=[vmem] * 6 + [smem],
        out_specs=vmem,
        scratch_shapes=[
            pltpu.VMEM((lanes, n_out + 4 * hw), jnp.bfloat16),
            pltpu.VMEM((reach_y, views * planes, lanes), jnp.bfloat16),
            pltpu.VMEM((reach_y, reach_x * planes, views * planes), jnp.bfloat16),
            pltpu.VMEM((views * planes, n_mid), jnp.bfloat16),
        ],
    )(*[pltpu.with_memory_space_constraint(x, pltpu.VMEM) for x in (start, before, after, blur_b, corr_b, meas2)],
      background)
    return est


def solution(mesh):
    in_specs = (P(None, None, ("parts", "gy"), None), P(None, ("parts", "gy"), None), P(), P())
    out_specs = P(None, ("parts", "gy"), None)
    return jax.shard_map(local, mesh=mesh, in_specs=in_specs, out_specs=out_specs, check_vma=False)
```
